256 devices in a mesh: clip: 2 (over y_lo), fsdp: 8 (over x, core), sp: 16 (over z, y_hi).
Axes of the slice: x: 4, y: 4 (y_hi: 2, y_lo: 2; y = y_hi * 2 + y_lo), z: 8, core: 2. Of those that a mesh axis runs over, the one named last changes fastest.
Arguments:
- queries: bfloat16 [16, 2048, 2560], P(('clip', 'fsdp'), 'sp'), may hold values from -36 to 36
- key_vectors: bfloat16 [16, 2048, 2560], P(('clip', 'fsdp'), 'sp'), may hold values from -36 to 36
- value_vectors: bfloat16 [16, 2048, 2560], P(('clip', 'fsdp'), 'sp'), may hold values from -6 to 6
- windows: int32 [20, 3], replicated, may hold values from 0 to 1, as said below
- gain_query: float32 [2560], P('fsdp'), may hold values from 0.25 to 1.75
- gain_key: float32 [2560], P('fsdp'), may hold values from 0.25 to 1.75
- grad_output: bfloat16 [16, 2048, 2560], P(('clip', 'fsdp'), 'sp'), may hold values from -18 to 18
Outputs:
- attended: bfloat16 [16, 2048, 2560], P(('clip', 'fsdp'), 'sp')
- grad_queries: bfloat16 [16, 2048, 2560], P(('clip', 'fsdp'), 'sp')
- grad_keys: bfloat16 [16, 2048, 2560], P(('clip', 'fsdp'), 'sp')
- grad_values: bfloat16 [16, 2048, 2560], P(('clip', 'fsdp'), 'sp')
- grad_gain_query: float32 [2560], P('fsdp')
- grad_gain_key: float32 [2560], P('fsdp')
The draws below stay inside these ranges and needn't reach their ends.
Inputs may be any that keep to these rules, and one draw needn't show every extreme that they name: windows[h] holds head h's radius along frames, height and width; some head has radius 1 along all three.
All inputs are finite; a program needn't handle non-finite values.
Results may differ from the reference program's by a relative error of at most 0.009.
The reference program's roundings to bfloat16 on the way count: a program that leaves them out, or rounds other values in their place, can miss the bound.
Values may be sent and summed in bfloat16 or wider, within the bound.
No kernel may reach another device: no remote copies, remote signals or barrier semaphores. Data moves between devices by JAX's collectives and lax.ppermute only.
A program may use at most 64 MiB of HBM per device.

```python
import math
import jax
import jax.numpy as jnp
from jax import lax

HEADS = 20
HEAD = 128
TILE = 64
GW = 1
HD = 2560
TOK = 128
TOKENS_CLIP = 2048
CLIPS = 16
ALLTOK = 32768
N_SP = 16


def spread_scales(key):
    col_key, row_key = jax.random.split(key)
    columns = jnp.exp(jax.random.uniform(col_key, (HD,), jnp.float32, math.log(0.3), math.log(3.0)))
    row_scale = jnp.exp(jax.random.uniform(row_key, (CLIPS, TOKENS_CLIP, 1), jnp.float32, math.log(0.3), math.log(3.0)))
    return columns * row_scale


def base_field(key):
    shape = (CLIPS, TOKENS_CLIP, HD)
    noise_key, scale_key = jax.random.split(key)
    field = jax.random.truncated_normal(noise_key, -4.0, 4.0, shape, jnp.float32)
    return field * spread_scales(scale_key)


def draw_queries(key, part):
    field = base_field(jax.random.fold_in(key, 1))
    return field.astype(jnp.bfloat16)


def draw_key_vectors(key, part):
    field = base_field(jax.random.fold_in(key, 2))
    return field.astype(jnp.bfloat16)


def draw_windows(key, part):
    radius_key, wide_key = jax.random.split(key)
    radius = jax.random.randint(radius_key, (HEADS, 3), 0, 2)
    widest = jax.random.randint(wide_key, (), 0, HEADS)
    return jnp.where((jnp.arange(HEADS) == widest)[:, None], 1, radius).astype(jnp.int32)


def draw_grad_output(key, part):
    shape = (CLIPS, TOKENS_CLIP, HD)
    noise_key = jax.random.fold_in(key, 0)
    rising_row = 1.0 + 2.0 * jnp.arange(TOKENS_CLIP, dtype=jnp.float32)[None, :, None] / (TOKENS_CLIP - 1)
    rising_clip = 1.0 + 2.0 * jnp.arange(CLIPS, dtype=jnp.float32)[:, None, None] / (CLIPS - 1)
    field = 0.5 * jax.random.truncated_normal(noise_key, -4.0, 4.0, shape, jnp.float32)
    return (field * rising_row * rising_clip).astype(jnp.bfloat16)


def level_of(key, shape, shards, smallest, largest):
    loudness, own = 1.0, jax.random.fold_in(key, 6)
    for axis_at, shards_of in shards:
        draws = jnp.exp(jax.random.uniform(jax.random.fold_in(own, axis_at), (shards_of,), jnp.float32, smallest / len(shards), largest / len(shards)))
        loudness = loudness * jnp.repeat(draws, shape[axis_at] // shards_of).reshape([-1 if axis == axis_at else 1 for axis in range(len(shape))])
    return loudness


def noise(key, extent, scale, bound, cuts=(), held_as=jnp.bfloat16):
    entries = jax.random.normal(key, extent, jnp.float32) * scale
    if len(cuts) > 0:
        entries = level_of(key, extent, cuts, -0.22, 0.18) * entries
    return jnp.clip(entries, min=-bound, max=bound).astype(held_as)


def setup_inputs(seed: int = 0) -> dict:
    arg_keys = jax.random.split(jax.random.key(seed), 8)
    queries = draw_queries(jax.random.fold_in(arg_keys[7], 71), 0)
    key_vectors = draw_key_vectors(jax.random.fold_in(arg_keys[7], 71), 0)
    value_vectors = noise(arg_keys[2], (CLIPS, TOKENS_CLIP, HD), 1.0, 6.0, ((0, 16), (1, 16)))
    windows = draw_windows(jax.random.fold_in(arg_keys[7], 71), 0)
    gain_query = jnp.clip(1.0 + 0.15 * jax.random.normal(arg_keys[4], (HD,), jnp.float32), 0.25, 1.75)
    gain_key = jnp.clip(1.0 + 0.15 * jax.random.normal(arg_keys[5], (HD,), jnp.float32), 0.25, 1.75)
    grad_output = draw_grad_output(jax.random.fold_in(arg_keys[7], 71), 0)
    return dict(queries=queries, key_vectors=key_vectors, value_vectors=value_vectors, windows=windows, gain_query=gain_query, gain_key=gain_key, grad_output=grad_output)


EPSILON = 1e-06
NEG_FILL = -1e+30

def product(pattern, left_side, right_side):
    return jnp.einsum(pattern, left_side.astype(jnp.float32), right_side.astype(jnp.float32))

def tile_place(position):
    tile_number = position // TILE
    return (tile_number // GW, tile_number % GW)

def window_mask(radius, query_time, query_col, query_row, key_time, key_col, key_row, key_valid):
    apart_time = jnp.abs(query_time[:, None] - key_time[None, :])
    apart_col = jnp.abs(query_col[:, None] - key_col[None, :])
    apart_row = jnp.abs(query_row[:, None] - key_row[None, :])
    inside = apart_time[None] <= radius[:, 0, None, None]
    inside = inside & (apart_row[None] <= radius[:, 1, None, None])
    inside = inside & (apart_col[None] <= radius[:, 2, None, None])
    return inside & key_valid[None, None, :]

def normalize(raw_rows, gain_full):
    as_float = raw_rows.astype(jnp.float32)
    inverse = lax.rsqrt(lax.optimization_barrier(jnp.mean(as_float * as_float, axis=-1, keepdims=True)) + EPSILON)
    return (as_float, inverse, (as_float * inverse * gain_full).astype(jnp.bfloat16))

def normalize_back(as_float, inverse, gain_full, d_normed):
    scaled = gain_full * d_normed
    inner = lax.optimization_barrier(jnp.mean(scaled * as_float, axis=-1, keepdims=True))
    d_raw = inverse * scaled - as_float * (inverse * inverse * inverse) * inner
    return (d_raw.astype(jnp.bfloat16), lax.optimization_barrier(jnp.sum(d_normed * as_float * inverse, axis=0)))

def forward_group(query_part, key_part, value_part, allowed, scaling):
    scores = product('qhd,khd->hqk', query_part, key_part) * scaling
    scores = jnp.where(allowed, scores, NEG_FILL)
    row_max = lax.optimization_barrier(jnp.max(scores, axis=2, keepdims=True))
    row_sum = lax.optimization_barrier(jnp.sum(jnp.exp(scores - row_max), axis=2, keepdims=True))
    log_sum = row_max + jnp.log(row_sum)
    weights = jnp.exp(scores - log_sum)
    weights_low = weights.astype(jnp.bfloat16)
    mixed = product('hqk,khd->qhd', weights_low, value_part)
    return (weights, weights_low, mixed, log_sum[:, :, 0])

def score_grads(weights, output_part, value_part, delta, scaling):
    d_weights = product('qhd,khd->hqk', output_part, value_part)
    return (weights * (d_weights - delta[:, :, None]) * scaling).astype(jnp.bfloat16)

def rounded(values):
    return lax.optimization_barrier(values.astype(jnp.bfloat16)).astype(jnp.float32)

def reference(queries, key_vectors, value_vectors, windows, gain_query, gain_key, grad_output):
    scaling = HEAD ** (-0.5)
    width = HEADS * HEAD
    group_size = 4 if HEADS % 4 == 0 else HEADS
    slab_count = N_SP
    tok_rows = TOK
    own_pos = jnp.arange(tok_rows, dtype=jnp.int32)
    own_time, own_col = tile_place(own_pos)
    ext_pos = jnp.arange(3 * tok_rows, dtype=jnp.int32)
    ext_time, ext_col = tile_place(ext_pos % tok_rows)

    def one_clip(clip_items):
        query_in, key_in, value_in, output_in = clip_items
        q_float, q_inverse, q_normed = normalize(query_in, gain_query)
        k_float, k_inverse, k_normed = normalize(key_in, gain_key)
        pad_spec = ((1, 1), (0, 0), (0, 0), (0, 0))
        key_pad = jnp.pad(k_normed.reshape(slab_count, tok_rows, HEADS, HEAD), pad_spec)
        value_pad = jnp.pad(value_in.reshape(slab_count, tok_rows, HEADS, HEAD), pad_spec)
        query_slabs = q_normed.reshape(slab_count, tok_rows, HEADS, HEAD)
        output_slabs = output_in.reshape(slab_count, tok_rows, HEADS, HEAD)

        def one_slab(slab_index):
            key_ext = lax.dynamic_slice_in_dim(key_pad, slab_index, 3, 0).reshape(3 * tok_rows, HEADS, HEAD)
            value_ext = lax.dynamic_slice_in_dim(value_pad, slab_index, 3, 0).reshape(3 * tok_rows, HEADS, HEAD)
            query_heads = query_slabs[slab_index]
            output_heads = output_slabs[slab_index]
            own_row = jnp.zeros((tok_rows,), jnp.int32) + slab_index
            ext_row = slab_index - 1 + ext_pos // tok_rows
            ext_valid = (ext_row >= 0) & (ext_row < slab_count)
            mixed_parts, dq_parts, dk_parts, dv_parts = ([], [], [], [])
            for first_head in range(0, HEADS, group_size):
                head_range = slice(first_head, first_head + group_size)
                allowed = window_mask(windows[head_range], own_time, own_col, own_row, ext_time, ext_col, ext_row, ext_valid)
                weights, weights_low, mixed, log_sum = forward_group(query_heads[:, head_range], key_ext[:, head_range], value_ext[:, head_range], allowed, scaling)
                delta = lax.optimization_barrier(jnp.sum(output_heads[:, head_range].astype(jnp.float32) * mixed, axis=2)).T
                d_scores = score_grads(weights, output_heads[:, head_range], value_ext[:, head_range], delta, scaling)
                dq_parts.append(product('hqk,khd->qhd', d_scores, key_ext[:, head_range]))
                dk_parts.append(product('hqk,qhd->khd', d_scores, query_heads[:, head_range]))
                dv_parts.append(product('hqk,qhd->khd', weights_low, output_heads[:, head_range]))
                mixed_parts.append(mixed)
            mixed_all = jnp.concatenate(mixed_parts, axis=1).reshape(tok_rows, width)
            dq_all = jnp.concatenate(dq_parts, axis=1).reshape(tok_rows, width)
            dk_all = jnp.concatenate(dk_parts, axis=1).reshape(3, tok_rows, width)
            dv_all = jnp.concatenate(dv_parts, axis=1).reshape(3, tok_rows, width)
            return (mixed_all, dq_all, dk_all, dv_all)
        mixed, dq_normed, dk_ext, dv_ext = lax.map(one_slab, jnp.arange(slab_count, dtype=jnp.int32))
        zero_slab = jnp.zeros((1, tok_rows, width), jnp.float32)
        dk_normed = dk_ext[:, 1] + jnp.concatenate([rounded(dk_ext[1:, 0]), zero_slab], axis=0) + jnp.concatenate([zero_slab, rounded(dk_ext[:-1, 2])], axis=0)
        dv_total = dv_ext[:, 1] + jnp.concatenate([rounded(dv_ext[1:, 0]), zero_slab], axis=0) + jnp.concatenate([zero_slab, rounded(dv_ext[:-1, 2])], axis=0)
        dq_out, dg_query = normalize_back(q_float, q_inverse, gain_query, dq_normed.reshape(-1, width))
        dk_out, dg_key = normalize_back(k_float, k_inverse, gain_key, dk_normed.reshape(-1, width))
        return (mixed.reshape(-1, width).astype(jnp.bfloat16), dq_out, dk_out, dv_total.reshape(-1, width).astype(jnp.bfloat16), dg_query, dg_key)
    results = lax.map(one_clip, (queries, key_vectors, value_vectors, grad_output))
    factor = ALLTOK ** (-0.5)
    return (results[0], results[1], results[2], results[3], lax.optimization_barrier(jnp.sum(results[4], axis=0)) * factor, lax.optimization_barrier(jnp.sum(results[5], axis=0)) * factor)
```

```python
import jax
import jax.numpy as jnp
from jax import lax
from jax.sharding import PartitionSpec as P

HEADS = 20
HEAD = 128
TILE = 64
GW = 1


EPSILON = 1e-06
NEG_FILL = -1e30


def padded(block, sides, width):
    for axis, dim in sides:
        count = lax.axis_size(axis)
        forward = [(i, i + 1) for i in range(count - 1)]
        backward = [(target, source) for source, target in forward]
        low = lax.ppermute(
            lax.slice_in_dim(block, block.shape[dim] - width, None, axis=dim), axis, forward
        )
        high = lax.ppermute(lax.slice_in_dim(block, 0, width, axis=dim), axis, backward)
        block = jnp.concatenate([low, block, high], axis=dim)
    return block


def butterfly_gather(block, axis):
    count = lax.axis_size(axis)
    if count & (count - 1):
        return lax.all_gather(block, axis, axis=block.ndim - 1, tiled=True)
    me = lax.axis_index(axis)
    step = 1
    while step < count:
        other = lax.ppermute(block, axis, [(i, i ^ step) for i in range(count)])
        low_first = (me // step) % 2 == 0
        block = jnp.where(
            low_first,
            jnp.concatenate([block, other], axis=-1),
            jnp.concatenate([other, block], axis=-1),
        )
        step *= 2
    return block


def butterfly_sum(total, axes):
    for axis in axes:
        count = lax.axis_size(axis)
        if count & (count - 1):
            total = lax.psum(total, axis)
            continue
        step = 1
        while step < count:
            total = total + lax.ppermute(total, axis, [(i, i ^ step) for i in range(count)])
            step *= 2
    return total


def passed_along(block, axis, distance):
    devices = range(lax.axis_size(axis))
    route = [(i - distance, i) for i in devices if i - distance in devices]
    return lax.ppermute(block, axis, route)


def product(pattern, left_side, right_side):
    return jnp.einsum(pattern, left_side, right_side, preferred_element_type=jnp.float32)


def tile_place(position):
    tile_number = position // TILE
    return (tile_number // GW, tile_number % GW)


def window_mask(radius, query_time, query_col, query_row, key_time, key_col, key_row, key_valid):
    apart_time = jnp.abs(query_time[:, None] - key_time[None, :])
    apart_col = jnp.abs(query_col[:, None] - key_col[None, :])
    apart_row = jnp.abs(query_row[:, None] - key_row[None, :])
    inside = apart_time[None] <= radius[:, 0, None, None]
    inside = inside & (apart_row[None] <= radius[:, 1, None, None])
    inside = inside & (apart_col[None] <= radius[:, 2, None, None])
    return inside & key_valid[None, None, :]


def normalize(raw_rows, gain_full):
    as_float = raw_rows.astype(jnp.float32)
    inverse = lax.rsqrt(jnp.mean(as_float * as_float, axis=-1, keepdims=True) + EPSILON)
    return (as_float, inverse, (as_float * inverse * gain_full).astype(jnp.bfloat16))


def normalize_back(as_float, inverse, gain_full, d_normed):
    scaled = gain_full * d_normed
    inner = jnp.mean(scaled * as_float, axis=-1, keepdims=True)
    d_raw = inverse * scaled - as_float * (inverse * inverse * inverse) * inner
    return (d_raw.astype(jnp.bfloat16), jnp.sum(d_normed * as_float * inverse, axis=0))


def forward_group(query_part, key_part, value_part, allowed, scaling):
    scores = product("qhd,khd->hqk", query_part, key_part) * scaling
    scores = jnp.where(allowed, scores, NEG_FILL)
    row_max = jnp.max(scores, axis=2, keepdims=True)
    row_sum = jnp.sum(jnp.exp(scores - row_max), axis=2, keepdims=True)
    log_sum = row_max + jnp.log(row_sum)
    weights = jnp.exp(scores - log_sum)
    weights_low = weights.astype(jnp.bfloat16)
    mixed = product("hqk,khd->qhd", weights_low, value_part)
    return (weights, weights_low, mixed, log_sum[:, :, 0])


def score_grads(weights, output_part, value_part, delta, scaling):
    d_weights = product("qhd,khd->hqk", output_part, value_part)
    return (weights * (d_weights - delta[:, :, None]) * scaling).astype(jnp.bfloat16)


def shards(queries, key_vectors, value_vectors, windows, gain_query, gain_key, grad_output):
    tok_rows = queries.shape[1]
    width = HEADS * HEAD
    extended = padded(jnp.stack([key_vectors[0], value_vectors[0]]), (("sp", 1),), tok_rows)
    gains = butterfly_gather(jnp.stack([gain_query, gain_key]), "fsdp")
    gain_q_full, gain_k_full = gains[0], gains[1]
    my_index = lax.axis_index("sp")
    sp_count = lax.axis_size("sp")
    scaling = HEAD ** (-0.5)
    group_size = 4
    q_float, q_inverse, q_normed = normalize(queries[0], gain_q_full)
    k_float, k_inverse, k_normed = normalize(key_vectors[0], gain_k_full)
    lo_float, lo_inverse, lo_normed = normalize(extended[0, :tok_rows], gain_k_full)
    hi_float, hi_inverse, hi_normed = normalize(extended[0, 2 * tok_rows :], gain_k_full)
    value_local = value_vectors[0]
    output_local = grad_output[0]
    key_ext = jnp.concatenate([lo_normed, k_normed, hi_normed]).reshape(3 * tok_rows, HEADS, HEAD)
    value_ext = extended[1].reshape(3 * tok_rows, HEADS, HEAD)
    query_heads = q_normed.reshape(tok_rows, HEADS, HEAD)
    output_heads = output_local.reshape(tok_rows, HEADS, HEAD)
    own_pos = jnp.arange(tok_rows, dtype=jnp.int32)
    own_time, own_col = tile_place(own_pos)
    own_row = jnp.zeros((tok_rows,), jnp.int32) + my_index
    ext_pos = jnp.arange(3 * tok_rows, dtype=jnp.int32)
    ext_time, ext_col = tile_place(ext_pos % tok_rows)
    ext_row = my_index - 1 + ext_pos // tok_rows
    ext_valid = (ext_row >= 0) & (ext_row < sp_count)
    middle = slice(tok_rows, 2 * tok_rows)
    mixed_parts, dq_parts, dk_parts, dv_parts, stat_parts = ([], [], [], [], [])
    for first_head in range(0, HEADS, group_size):
        head_range = slice(first_head, first_head + group_size)
        allowed = window_mask(
            windows[head_range], own_time, own_col, own_row, ext_time, ext_col, ext_row, ext_valid
        )
        weights, weights_low, mixed, log_sum = forward_group(
            query_heads[:, head_range],
            key_ext[:, head_range],
            value_ext[:, head_range],
            allowed,
            scaling,
        )
        delta = jnp.sum(output_heads[:, head_range] * mixed, axis=2).T
        d_scores = score_grads(
            weights, output_heads[:, head_range], value_ext[:, head_range], delta, scaling
        )
        dq_parts.append(product("hqk,khd->qhd", d_scores, key_ext[:, head_range]))
        dk_parts.append(product("hqk,qhd->khd", d_scores, query_heads[:, head_range]))
        dv_parts.append(product("hqk,qhd->khd", weights_low, output_heads[:, head_range]))
        mixed_parts.append(mixed)
    mixed_all = jnp.concatenate(mixed_parts, axis=1).reshape(tok_rows, width)
    dq_normed = jnp.concatenate(dq_parts, axis=1).reshape(tok_rows, width)
    dk_all = jnp.concatenate(dk_parts, axis=1).reshape(-1, width)
    dv_all = jnp.concatenate(dv_parts, axis=1).reshape(-1, width)
    lower_send = jnp.stack([dk_all[:tok_rows], dv_all[:tok_rows]]).astype(jnp.bfloat16)
    upper_send = jnp.stack([dk_all[2 * tok_rows :], dv_all[2 * tok_rows :]]).astype(jnp.bfloat16)
    lower = passed_along(lower_send, "sp", -1).astype(jnp.float32)
    upper = passed_along(upper_send, "sp", 1).astype(jnp.float32)
    dk_normed = dk_all[middle] + lower[0] + upper[0]
    dv_total = dv_all[middle] + lower[1] + upper[1]
    dq_out, dg_query = normalize_back(q_float, q_inverse, gain_q_full, dq_normed)
    dk_out, _ = normalize_back(k_float, k_inverse, gain_k_full, dk_normed)
    dg_key = (
        jnp.sum(dk_all[middle] * k_float * k_inverse, axis=0)
        + jnp.sum(lower_send[0].astype(jnp.float32) * lo_float * lo_inverse, axis=0)
        + jnp.sum(upper_send[0].astype(jnp.float32) * hi_float * hi_inverse, axis=0)
    )
    all_tokens = tok_rows * sp_count * lax.axis_size("clip") * lax.axis_size("fsdp")
    factor = all_tokens ** (-0.5)
    totals = butterfly_sum(jnp.stack([dg_query, dg_key]), ("fsdp", "clip", "sp"))
    share = gain_query.shape[0]
    totals = lax.dynamic_slice_in_dim(totals, lax.axis_index("fsdp") * share, share, axis=1)
    return (
        mixed_all.astype(jnp.bfloat16)[None],
        dq_out[None],
        dk_out[None],
        dv_total.astype(jnp.bfloat16)[None],
        totals[0] * factor,
        totals[1] * factor,
    )


def solution(mesh):
    return jax.shard_map(
        shards,
        mesh=mesh,
        in_specs=(
            P(("clip", "fsdp"), "sp", None),
            P(("clip", "fsdp"), "sp", None),
            P(("clip", "fsdp"), "sp", None),
            P(),
            P("fsdp"),
            P("fsdp"),
            P(("clip", "fsdp"), "sp", None),
        ),
        out_specs=(
            P(("clip", "fsdp"), "sp", None),
            P(("clip", "fsdp"), "sp", None),
            P(("clip", "fsdp"), "sp", None),
            P(("clip", "fsdp"), "sp", None),
            P("fsdp"),
            P("fsdp"),
        ),
        check_vma=False,
    )
```

```python
import jax
import jax.numpy as jnp
from jax import lax
from jax.sharding import PartitionSpec as P

HEADS = 20
HEAD = 128
TILE = 64
GW = 1


EPSILON = 1e-06
NEG_FILL = -1e30


def padded(block, sides, width):
    for axis, dim in sides:
        count = lax.axis_size(axis)
        forward = [(i, i + 1) for i in range(count - 1)]
        backward = [(target, source) for source, target in forward]
        low = lax.ppermute(
            lax.slice_in_dim(block, block.shape[dim] - width, None, axis=dim), axis, forward
        )
        high = lax.ppermute(lax.slice_in_dim(block, 0, width, axis=dim), axis, backward)
        block = jnp.concatenate([low, block, high], axis=dim)
    return block


def butterfly_gather(block, axis):
    count = lax.axis_size(axis)
    if count & (count - 1):
        return lax.all_gather(block, axis, axis=block.ndim - 1, tiled=True)
    me = lax.axis_index(axis)
    step = 1
    while step < count:
        other = lax.ppermute(block, axis, [(i, i ^ step) for i in range(count)])
        low_first = (me // step) % 2 == 0
        block = jnp.where(
            low_first,
            jnp.concatenate([block, other], axis=-1),
            jnp.concatenate([other, block], axis=-1),
        )
        step *= 2
    return block


def butterfly_sum(total, steps):
    for axis, bit in steps:
        count = lax.axis_size(axis)
        total = total + lax.ppermute(total, axis, [(i, i ^ bit) for i in range(count)])
    return total


def bits_of(axis_sizes):
    steps = []
    for axis, count in axis_sizes:
        bit = 1
        while bit < count:
            steps.append((axis, bit))
            bit *= 2
    return steps


def passed_along(block, axis, distance):
    devices = range(lax.axis_size(axis))
    route = [(i - distance, i) for i in devices if i - distance in devices]
    return lax.ppermute(block, axis, route)


def product(pattern, left_side, right_side):
    return jnp.einsum(pattern, left_side, right_side, preferred_element_type=jnp.float32)


def tile_place(position):
    tile_number = position // TILE
    return (tile_number // GW, tile_number % GW)


def window_mask(radius, query_time, query_col, query_row, key_time, key_col, key_row, key_valid):
    apart_time = jnp.abs(query_time[:, None] - key_time[None, :])
    apart_col = jnp.abs(query_col[:, None] - key_col[None, :])
    apart_row = jnp.abs(query_row[:, None] - key_row[None, :])
    inside = apart_time[None] <= radius[:, 0, None, None]
    inside = inside & (apart_row[None] <= radius[:, 1, None, None])
    inside = inside & (apart_col[None] <= radius[:, 2, None, None])
    return inside & key_valid[None, None, :]


def normalize(raw_rows, gain_full):
    as_float = raw_rows.astype(jnp.float32)
    inverse = lax.rsqrt(jnp.mean(as_float * as_float, axis=-1, keepdims=True) + EPSILON)
    return (as_float, inverse, (as_float * inverse * gain_full).astype(jnp.bfloat16))


def normalize_back(as_float, inverse, gain_full, d_normed):
    scaled = gain_full * d_normed
    inner = jnp.mean(scaled * as_float, axis=-1, keepdims=True)
    d_raw = inverse * scaled - as_float * (inverse * inverse * inverse) * inner
    return (d_raw.astype(jnp.bfloat16), jnp.sum(d_normed * as_float * inverse, axis=0))


def forward_group(query_part, key_part, value_part, allowed, scaling):
    scores = product("qhd,khd->hqk", query_part, key_part) * scaling
    scores = jnp.where(allowed, scores, NEG_FILL)
    row_max = jnp.max(scores, axis=2, keepdims=True)
    row_sum = jnp.sum(jnp.exp(scores - row_max), axis=2, keepdims=True)
    log_sum = row_max + jnp.log(row_sum)
    weights = jnp.exp(scores - log_sum)
    weights_low = weights.astype(jnp.bfloat16)
    mixed = product("hqk,khd->qhd", weights_low, value_part)
    return (weights, weights_low, mixed, log_sum[:, :, 0])


def score_grads(weights, output_part, value_part, delta, scaling):
    d_weights = product("qhd,khd->hqk", output_part, value_part)
    return (weights * (d_weights - delta[:, :, None]) * scaling).astype(jnp.bfloat16)


def shards(queries, key_vectors, value_vectors, windows, gain_query, gain_key, grad_output):
    tok_rows = queries.shape[1]
    width = HEADS * HEAD
    extended = padded(jnp.stack([key_vectors[0], value_vectors[0]]), (("sp", 1),), tok_rows)
    gains = butterfly_gather(jnp.stack([gain_query, gain_key]), "fsdp")
    gain_q_full, gain_k_full = gains[0], gains[1]
    my_index = lax.axis_index("sp")
    sp_count = lax.axis_size("sp")
    scaling = HEAD ** (-0.5)
    group_size = 4
    q_float, q_inverse, q_normed = normalize(queries[0], gain_q_full)
    k_float, k_inverse, k_normed = normalize(key_vectors[0], gain_k_full)
    lo_float, lo_inverse, lo_normed = normalize(extended[0, :tok_rows], gain_k_full)
    hi_float, hi_inverse, hi_normed = normalize(extended[0, 2 * tok_rows :], gain_k_full)
    value_local = value_vectors[0]
    output_local = grad_output[0]
    key_ext = jnp.concatenate([lo_normed, k_normed, hi_normed]).reshape(3 * tok_rows, HEADS, HEAD)
    value_ext = extended[1].reshape(3 * tok_rows, HEADS, HEAD)
    query_heads = q_normed.reshape(tok_rows, HEADS, HEAD)
    output_heads = output_local.reshape(tok_rows, HEADS, HEAD)
    own_pos = jnp.arange(tok_rows, dtype=jnp.int32)
    own_time, own_col = tile_place(own_pos)
    own_row = jnp.zeros((tok_rows,), jnp.int32) + my_index
    ext_pos = jnp.arange(3 * tok_rows, dtype=jnp.int32)
    ext_time, ext_col = tile_place(ext_pos % tok_rows)
    ext_row = my_index - 1 + ext_pos // tok_rows
    ext_valid = (ext_row >= 0) & (ext_row < sp_count)
    middle = slice(tok_rows, 2 * tok_rows)
    mixed_parts, dq_parts, dk_parts, dv_parts, stat_parts = ([], [], [], [], [])
    for first_head in range(0, HEADS, group_size):
        head_range = slice(first_head, first_head + group_size)
        allowed = window_mask(
            windows[head_range], own_time, own_col, own_row, ext_time, ext_col, ext_row, ext_valid
        )
        weights, weights_low, mixed, log_sum = forward_group(
            query_heads[:, head_range],
            key_ext[:, head_range],
            value_ext[:, head_range],
            allowed,
            scaling,
        )
        delta = jnp.sum(output_heads[:, head_range] * mixed, axis=2).T
        d_scores = score_grads(
            weights, output_heads[:, head_range], value_ext[:, head_range], delta, scaling
        )
        dq_parts.append(product("hqk,khd->qhd", d_scores, key_ext[:, head_range]))
        dk_parts.append(product("hqk,qhd->khd", d_scores, query_heads[:, head_range]))
        dv_parts.append(product("hqk,qhd->khd", weights_low, output_heads[:, head_range]))
        mixed_parts.append(mixed)
    mixed_all = jnp.concatenate(mixed_parts, axis=1).reshape(tok_rows, width)
    dq_normed = jnp.concatenate(dq_parts, axis=1).reshape(tok_rows, width)
    dk_all = jnp.concatenate(dk_parts, axis=1).reshape(-1, width)
    dv_all = jnp.concatenate(dv_parts, axis=1).reshape(-1, width)
    lower_send = jnp.stack([dk_all[:tok_rows], dv_all[:tok_rows]]).astype(jnp.bfloat16)
    upper_send = jnp.stack([dk_all[2 * tok_rows :], dv_all[2 * tok_rows :]]).astype(jnp.bfloat16)
    lower = passed_along(lower_send, "sp", -1).astype(jnp.float32)
    upper = passed_along(upper_send, "sp", 1).astype(jnp.float32)
    dk_normed = dk_all[middle] + lower[0] + upper[0]
    dv_total = dv_all[middle] + lower[1] + upper[1]
    dq_out, dg_query = normalize_back(q_float, q_inverse, gain_q_full, dq_normed)
    dk_out, _ = normalize_back(k_float, k_inverse, gain_k_full, dk_normed)
    lower_held, upper_held, dg_query = lax.optimization_barrier((lower_send, upper_send, dg_query))
    dg_key = (
        jnp.sum(dk_all[middle] * k_float * k_inverse, axis=0)
        + jnp.sum(lower_held[0].astype(jnp.float32) * lo_float * lo_inverse, axis=0)
        + jnp.sum(upper_held[0].astype(jnp.float32) * hi_float * hi_inverse, axis=0)
    )
    all_tokens = tok_rows * sp_count * lax.axis_size("clip") * lax.axis_size("fsdp")
    factor = all_tokens ** (-0.5)
    sizes = {axis: lax.axis_size(axis) for axis in ("fsdp", "clip", "sp")}
    partial_sums = jnp.stack([dg_query, dg_key])
    if all(count & (count - 1) == 0 for count in sizes.values()):
        steps = bits_of([("fsdp", sizes["fsdp"])])
        steps += [("sp", bit) for _, bit in bits_of([("sp", sizes["sp"])]) if bit > 1]
        steps += bits_of([("clip", sizes["clip"])]) + [("sp", 1)] * (sizes["sp"] > 1)
        totals = butterfly_sum(partial_sums, steps)
    else:
        totals = lax.psum(partial_sums, ("fsdp", "clip", "sp"))
    share = gain_query.shape[0]
    totals = lax.dynamic_slice_in_dim(totals, lax.axis_index("fsdp") * share, share, axis=1)
    return (
        mixed_all.astype(jnp.bfloat16)[None],
        dq_out[None],
        dk_out[None],
        dv_total.astype(jnp.bfloat16)[None],
        totals[0] * factor,
        totals[1] * factor,
    )


def solution(mesh):
    return jax.shard_map(
        shards,
        mesh=mesh,
        in_specs=(
            P(("clip", "fsdp"), "sp", None),
            P(("clip", "fsdp"), "sp", None),
            P(("clip", "fsdp"), "sp", None),
            P(),
            P("fsdp"),
            P("fsdp"),
            P(("clip", "fsdp"), "sp", None),
        ),
        out_specs=(
            P(("clip", "fsdp"), "sp", None),
            P(("clip", "fsdp"), "sp", None),
            P(("clip", "fsdp"), "sp", None),
            P(("clip", "fsdp"), "sp", None),
            P("fsdp"),
            P("fsdp"),
        ),
        check_vma=False,
    )
```

```python
import jax
import jax.numpy as jnp
from jax import lax
from jax.sharding import PartitionSpec as P

HEADS = 20
HEAD = 128
TILE = 64
GW = 1


EPSILON = 1e-06
NEG_FILL = -1e30


def padded(block, sides, width):
    for axis, dim in sides:
        count = lax.axis_size(axis)
        forward = [(i, i + 1) for i in range(count - 1)]
        backward = [(target, source) for source, target in forward]
        low = lax.ppermute(
            lax.slice_in_dim(block, block.shape[dim] - width, None, axis=dim), axis, forward
        )
        high = lax.ppermute(lax.slice_in_dim(block, 0, width, axis=dim), axis, backward)
        block = jnp.concatenate([low, block, high], axis=dim)
    return block


def butterfly_gather(block, axis):
    count = lax.axis_size(axis)
    if count & (count - 1):
        return lax.all_gather(block, axis, axis=block.ndim - 1, tiled=True)
    me = lax.axis_index(axis)
    step = 1
    while step < count:
        other = lax.ppermute(block, axis, [(i, i ^ step) for i in range(count)])
        low_first = (me // step) % 2 == 0
        block = jnp.where(
            low_first,
            jnp.concatenate([block, other], axis=-1),
            jnp.concatenate([other, block], axis=-1),
        )
        step *= 2
    return block


def butterfly_sum(total, steps):
    for axis, bit in steps:
        count = lax.axis_size(axis)
        total = total + lax.ppermute(total, axis, [(i, i ^ bit) for i in range(count)])
    return total


def bits_of(axis_sizes):
    steps = []
    for axis, count in axis_sizes:
        bit = 1
        while bit < count:
            steps.append((axis, bit))
            bit *= 2
    return steps


def passed_along(block, axis, distance):
    devices = range(lax.axis_size(axis))
    route = [(i - distance, i) for i in devices if i - distance in devices]
    return lax.ppermute(block, axis, route)


def product(pattern, left_side, right_side):
    return jnp.einsum(pattern, left_side, right_side, preferred_element_type=jnp.float32)


def tile_place(position):
    tile_number = position // TILE
    return (tile_number // GW, tile_number % GW)


def window_mask(radius, query_time, query_col, query_row, key_time, key_col, key_row, key_valid):
    apart_time = jnp.abs(query_time[:, None] - key_time[None, :])
    apart_col = jnp.abs(query_col[:, None] - key_col[None, :])
    apart_row = jnp.abs(query_row[:, None] - key_row[None, :])
    inside = apart_time[None] <= radius[:, 0, None, None]
    inside = inside & (apart_row[None] <= radius[:, 1, None, None])
    inside = inside & (apart_col[None] <= radius[:, 2, None, None])
    return inside & key_valid[None, None, :]


def normalize(raw_rows, gain_full):
    as_float = raw_rows.astype(jnp.float32)
    inverse = lax.rsqrt(jnp.mean(as_float * as_float, axis=-1, keepdims=True) + EPSILON)
    return (as_float, inverse, (as_float * inverse * gain_full).astype(jnp.bfloat16))


def normalize_back(as_float, inverse, gain_full, d_normed):
    scaled = gain_full * d_normed
    inner = jnp.mean(scaled * as_float, axis=-1, keepdims=True)
    d_raw = inverse * scaled - as_float * (inverse * inverse * inverse) * inner
    return (d_raw.astype(jnp.bfloat16), jnp.sum(d_normed * as_float * inverse, axis=0))


def forward_group(query_part, key_part, value_part, allowed, scaling):
    scores = product("qhd,khd->hqk", query_part, key_part) * scaling
    scores = jnp.where(allowed, scores, NEG_FILL)
    row_max = jnp.max(scores, axis=2, keepdims=True)
    row_sum = jnp.sum(jnp.exp(scores - row_max), axis=2, keepdims=True)
    log_sum = row_max + jnp.log(row_sum)
    weights = jnp.exp(scores - log_sum)
    weights_low = weights.astype(jnp.bfloat16)
    mixed = product("hqk,khd->qhd", weights_low, value_part)
    return (weights, weights_low, mixed, log_sum[:, :, 0])


def score_grads(weights, output_part, value_part, delta, scaling):
    d_weights = product("qhd,khd->hqk", output_part, value_part)
    return (weights * (d_weights - delta[:, :, None]) * scaling).astype(jnp.bfloat16)


def attend_chunk(query_heads, output_heads, key_ext, value_ext, windows, masks, scaling, group_size):
    own_time, own_col, own_row, ext_time, ext_col, ext_row, ext_valid = masks
    heads = query_heads.shape[1]
    mixed_parts, dq_parts, dk_parts, dv_parts = ([], [], [], [])
    for first_head in range(0, heads, group_size):
        head_range = slice(first_head, first_head + group_size)
        allowed = window_mask(
            windows[head_range], own_time, own_col, own_row, ext_time, ext_col, ext_row, ext_valid
        )
        weights, weights_low, mixed, log_sum = forward_group(
            query_heads[:, head_range],
            key_ext[:, head_range],
            value_ext[:, head_range],
            allowed,
            scaling,
        )
        delta = jnp.sum(output_heads[:, head_range] * mixed, axis=2).T
        d_scores = score_grads(
            weights, output_heads[:, head_range], value_ext[:, head_range], delta, scaling
        )
        dq_parts.append(product("hqk,khd->qhd", d_scores, key_ext[:, head_range]))
        dk_parts.append(product("hqk,qhd->khd", d_scores, query_heads[:, head_range]))
        dv_parts.append(product("hqk,qhd->khd", weights_low, output_heads[:, head_range]))
        mixed_parts.append(mixed)
    rows = query_heads.shape[0]
    width = heads * HEAD
    return (
        jnp.concatenate(mixed_parts, axis=1).reshape(rows, width),
        jnp.concatenate(dq_parts, axis=1).reshape(rows, width),
        jnp.concatenate(dk_parts, axis=1).reshape(-1, width),
        jnp.concatenate(dv_parts, axis=1).reshape(-1, width),
    )


def shards(queries, key_vectors, value_vectors, windows, gain_query, gain_key, grad_output):
    tok_rows = queries.shape[1]
    width = HEADS * HEAD
    bounds = (0, 8, HEADS) if HEADS == 20 else (0, HEADS)
    chunks = len(bounds) - 1
    group_size = 4
    key_raw = key_vectors[0]
    value_local = value_vectors[0]
    extended = [
        padded(
            jnp.stack([key_raw[:, bounds[c] * HEAD : bounds[c + 1] * HEAD],
                       value_local[:, bounds[c] * HEAD : bounds[c + 1] * HEAD]]),
            (("sp", 1),),
            tok_rows,
        )
        for c in range(chunks)
    ]
    k_float = key_raw.astype(jnp.float32)
    k_inverse = lax.rsqrt(jnp.mean(k_float * k_float, axis=-1, keepdims=True) + EPSILON)
    inverse_ext = padded(k_inverse, (("sp", 0),), tok_rows)
    lo_inverse, hi_inverse = inverse_ext[:tok_rows], inverse_ext[2 * tok_rows :]
    gains = butterfly_gather(jnp.stack([gain_query, gain_key]), "fsdp")
    gain_q_full, gain_k_full = gains[0], gains[1]
    my_index = lax.axis_index("sp")
    sp_count = lax.axis_size("sp")
    scaling = HEAD ** (-0.5)
    q_float, q_inverse, q_normed = normalize(queries[0], gain_q_full)
    k_normed = (k_float * k_inverse * gain_k_full).astype(jnp.bfloat16)
    output_local = grad_output[0]
    query_heads = q_normed.reshape(tok_rows, HEADS, HEAD)
    output_heads = output_local.reshape(tok_rows, HEADS, HEAD)
    own_pos = jnp.arange(tok_rows, dtype=jnp.int32)
    own_time, own_col = tile_place(own_pos)
    own_row = jnp.zeros((tok_rows,), jnp.int32) + my_index
    ext_pos = jnp.arange(3 * tok_rows, dtype=jnp.int32)
    ext_time, ext_col = tile_place(ext_pos % tok_rows)
    ext_row = my_index - 1 + ext_pos // tok_rows
    ext_valid = (ext_row >= 0) & (ext_row < sp_count)
    masks = (own_time, own_col, own_row, ext_time, ext_col, ext_row, ext_valid)
    middle = slice(tok_rows, 2 * tok_rows)
    results, received, near_dg = [], [], []
    for c in range(chunks):
        if c > 0:
            extended[c], held = lax.optimization_barrier((extended[c], sent))
        cols = slice(bounds[c] * HEAD, bounds[c + 1] * HEAD)
        heads = slice(bounds[c], bounds[c + 1])
        chunk_heads = bounds[c + 1] - bounds[c]
        lo_float = extended[c][0, :tok_rows].astype(jnp.float32)
        hi_float = extended[c][0, 2 * tok_rows :].astype(jnp.float32)
        gain_c = gain_k_full[cols]
        key_ext = jnp.concatenate([
            (lo_float * lo_inverse * gain_c).astype(jnp.bfloat16),
            k_normed[:, cols],
            (hi_float * hi_inverse * gain_c).astype(jnp.bfloat16),
        ]).reshape(3 * tok_rows, chunk_heads, HEAD)
        value_ext = extended[c][1].reshape(3 * tok_rows, chunk_heads, HEAD)
        mixed_c, dq_c, dk_c, dv_c = attend_chunk(
            query_heads[:, heads], output_heads[:, heads], key_ext, value_ext,
            windows[heads], masks, scaling, group_size,
        )
        lower_send = jnp.stack([dk_c[:tok_rows], dv_c[:tok_rows]]).astype(jnp.bfloat16)
        upper_send = jnp.stack([dk_c[2 * tok_rows :], dv_c[2 * tok_rows :]]).astype(jnp.bfloat16)
        received.append((passed_along(lower_send, "sp", -1), passed_along(upper_send, "sp", 1)))
        sent = (lower_send, upper_send)
        results.append((mixed_c, dq_c, dk_c[middle], dv_c[middle]))
        near_dg.append(
            jnp.sum(lower_send[0].astype(jnp.float32) * lo_float * lo_inverse, axis=0)
            + jnp.sum(upper_send[0].astype(jnp.float32) * hi_float * hi_inverse, axis=0)
        )
    mixed_all = jnp.concatenate([r[0] for r in results], axis=1)
    dq_normed = jnp.concatenate([r[1] for r in results], axis=1)
    dk_own = jnp.concatenate([r[2] for r in results], axis=1)
    dv_own = jnp.concatenate([r[3] for r in results], axis=1)
    lower = jnp.concatenate([r[0] for r in received], axis=2).astype(jnp.float32)
    upper = jnp.concatenate([r[1] for r in received], axis=2).astype(jnp.float32)
    dk_normed = dk_own + lower[0] + upper[0]
    dv_total = dv_own + lower[1] + upper[1]
    dq_out, dg_query = normalize_back(q_float, q_inverse, gain_q_full, dq_normed)
    dk_out, _ = normalize_back(k_float, k_inverse, gain_k_full, dk_normed)
    dg_key = jnp.sum(dk_own * k_float * k_inverse, axis=0) + jnp.concatenate(near_dg)
    all_tokens = tok_rows * sp_count * lax.axis_size("clip") * lax.axis_size("fsdp")
    factor = all_tokens ** (-0.5)
    sizes = {axis: lax.axis_size(axis) for axis in ("fsdp", "clip", "sp")}
    partial_sums = jnp.stack([dg_query, dg_key])
    if all(count & (count - 1) == 0 for count in sizes.values()):
        steps = bits_of([("fsdp", sizes["fsdp"])])
        steps += [("sp", bit) for _, bit in bits_of([("sp", sizes["sp"])]) if bit > 1]
        steps += bits_of([("clip", sizes["clip"])]) + [("sp", 1)] * (sizes["sp"] > 1)
        totals = butterfly_sum(partial_sums, steps)
    else:
        totals = lax.psum(partial_sums, ("fsdp", "clip", "sp"))
    share = gain_query.shape[0]
    totals = lax.dynamic_slice_in_dim(totals, lax.axis_index("fsdp") * share, share, axis=1)
    return (
        mixed_all.astype(jnp.bfloat16)[None],
        dq_out[None],
        dk_out[None],
        dv_total.astype(jnp.bfloat16)[None],
        totals[0] * factor,
        totals[1] * factor,
    )


def solution(mesh):
    return jax.shard_map(
        shards,
        mesh=mesh,
        in_specs=(
            P(("clip", "fsdp"), "sp", None),
            P(("clip", "fsdp"), "sp", None),
            P(("clip", "fsdp"), "sp", None),
            P(),
            P("fsdp"),
            P("fsdp"),
            P(("clip", "fsdp"), "sp", None),
        ),
        out_specs=(
            P(("clip", "fsdp"), "sp", None),
            P(("clip", "fsdp"), "sp", None),
            P(("clip", "fsdp"), "sp", None),
            P(("clip", "fsdp"), "sp", None),
            P("fsdp"),
            P("fsdp"),
        ),
        check_vma=False,
    )
```

```python
import jax
import jax.numpy as jnp
from jax import lax
from jax.sharding import PartitionSpec as P

HEADS = 20
HEAD = 128
TILE = 64
GW = 1


EPSILON = 1e-06
NEG_FILL = -1e30


def padded(block, sides, width):
    for axis, dim in sides:
        count = lax.axis_size(axis)
        forward = [(i, i + 1) for i in range(count - 1)]
        backward = [(target, source) for source, target in forward]
        low = lax.ppermute(
            lax.slice_in_dim(block, block.shape[dim] - width, None, axis=dim), axis, forward
        )
        high = lax.ppermute(lax.slice_in_dim(block, 0, width, axis=dim), axis, backward)
        block = jnp.concatenate([low, block, high], axis=dim)
    return block


def butterfly_gather(block, axis):
    count = lax.axis_size(axis)
    if count & (count - 1):
        return lax.all_gather(block, axis, axis=block.ndim - 1, tiled=True)
    me = lax.axis_index(axis)
    step = 1
    while step < count:
        other = lax.ppermute(block, axis, [(i, i ^ step) for i in range(count)])
        low_first = (me // step) % 2 == 0
        block = jnp.where(
            low_first,
            jnp.concatenate([block, other], axis=-1),
            jnp.concatenate([other, block], axis=-1),
        )
        step *= 2
    return block


def butterfly_sum(total, steps):
    for axis, bit in steps:
        count = lax.axis_size(axis)
        total = total + lax.ppermute(total, axis, [(i, i ^ bit) for i in range(count)])
    return total


def bits_of(axis_sizes):
    steps = []
    for axis, count in axis_sizes:
        bit = 1
        while bit < count:
            steps.append((axis, bit))
            bit *= 2
    return steps


def passed_along(block, axis, distance):
    devices = range(lax.axis_size(axis))
    route = [(i - distance, i) for i in devices if i - distance in devices]
    return lax.ppermute(block, axis, route)


def product(pattern, left_side, right_side):
    return jnp.einsum(pattern, left_side, right_side, preferred_element_type=jnp.float32)


def tile_place(position):
    tile_number = position // TILE
    return (tile_number // GW, tile_number % GW)


def window_mask(radius, query_time, query_col, query_row, key_time, key_col, key_row, key_valid):
    apart_time = jnp.abs(query_time[:, None] - key_time[None, :])
    apart_col = jnp.abs(query_col[:, None] - key_col[None, :])
    apart_row = jnp.abs(query_row[:, None] - key_row[None, :])
    inside = apart_time[None] <= radius[:, 0, None, None]
    inside = inside & (apart_row[None] <= radius[:, 1, None, None])
    inside = inside & (apart_col[None] <= radius[:, 2, None, None])
    return inside & key_valid[None, None, :]


def normalize(raw_rows, gain_full):
    as_float = raw_rows.astype(jnp.float32)
    inverse = lax.rsqrt(jnp.mean(as_float * as_float, axis=-1, keepdims=True) + EPSILON)
    return (as_float, inverse, (as_float * inverse * gain_full).astype(jnp.bfloat16))


def normalize_back(as_float, inverse, gain_full, d_normed):
    scaled = gain_full * d_normed
    inner = jnp.mean(scaled * as_float, axis=-1, keepdims=True)
    d_raw = inverse * scaled - as_float * (inverse * inverse * inverse) * inner
    return (d_raw.astype(jnp.bfloat16), jnp.sum(d_normed * as_float * inverse, axis=0))


def forward_group(query_part, key_part, value_part, allowed, scaling):
    scores = product("qhd,khd->hqk", query_part, key_part) * scaling
    scores = jnp.where(allowed, scores, NEG_FILL)
    row_max = jnp.max(scores, axis=2, keepdims=True)
    row_sum = jnp.sum(jnp.exp(scores - row_max), axis=2, keepdims=True)
    log_sum = row_max + jnp.log(row_sum)
    weights = jnp.exp(scores - log_sum)
    weights_low = weights.astype(jnp.bfloat16)
    mixed = product("hqk,khd->qhd", weights_low, value_part)
    return (weights, weights_low, mixed, log_sum[:, :, 0])


def score_grads(weights, output_part, value_part, delta, scaling):
    d_weights = product("qhd,khd->hqk", output_part, value_part)
    return (weights * (d_weights - delta[:, :, None]) * scaling).astype(jnp.bfloat16)


def attend_chunk(query_heads, output_heads, key_ext, value_ext, windows, masks, scaling, group_size):
    own_time, own_col, own_row, ext_time, ext_col, ext_row, ext_valid = masks
    heads = query_heads.shape[1]
    mixed_parts, dq_parts, dk_parts, dv_parts = ([], [], [], [])
    for first_head in range(0, heads, group_size):
        head_range = slice(first_head, first_head + group_size)
        allowed = window_mask(
            windows[head_range], own_time, own_col, own_row, ext_time, ext_col, ext_row, ext_valid
        )
        weights, weights_low, mixed, log_sum = forward_group(
            query_heads[:, head_range],
            key_ext[:, head_range],
            value_ext[:, head_range],
            allowed,
            scaling,
        )
        delta = jnp.sum(output_heads[:, head_range] * mixed, axis=2).T
        d_scores = score_grads(
            weights, output_heads[:, head_range], value_ext[:, head_range], delta, scaling
        )
        dq_parts.append(product("hqk,khd->qhd", d_scores, key_ext[:, head_range]))
        dk_parts.append(product("hqk,qhd->khd", d_scores, query_heads[:, head_range]))
        dv_parts.append(product("hqk,qhd->khd", weights_low, output_heads[:, head_range]))
        mixed_parts.append(mixed)
    rows = query_heads.shape[0]
    width = heads * HEAD
    return (
        jnp.concatenate(mixed_parts, axis=1).reshape(rows, width),
        jnp.concatenate(dq_parts, axis=1).reshape(rows, width),
        jnp.concatenate(dk_parts, axis=1).reshape(-1, width),
        jnp.concatenate(dv_parts, axis=1).reshape(-1, width),
    )


def shards(queries, key_vectors, value_vectors, windows, gain_query, gain_key, grad_output):
    tok_rows = queries.shape[1]
    width = HEADS * HEAD
    bounds = (0, 8, HEADS) if HEADS == 20 else (0, HEADS)
    chunks = len(bounds) - 1
    group_size = 4
    key_raw = key_vectors[0]
    value_local = value_vectors[0]
    extended = [
        padded(
            jnp.stack([key_raw[:, bounds[c] * HEAD : bounds[c + 1] * HEAD],
                       value_local[:, bounds[c] * HEAD : bounds[c + 1] * HEAD]]),
            (("sp", 1),),
            tok_rows,
        )
        for c in range(chunks)
    ]
    k_float = key_raw.astype(jnp.float32)
    k_inverse = lax.rsqrt(jnp.mean(k_float * k_float, axis=-1, keepdims=True) + EPSILON)
    inverse_ext = padded(k_inverse, (("sp", 0),), tok_rows)
    lo_inverse, hi_inverse = inverse_ext[:tok_rows], inverse_ext[2 * tok_rows :]
    gains = butterfly_gather(jnp.stack([gain_query, gain_key]), "fsdp")
    gain_q_full, gain_k_full = gains[0], gains[1]
    my_index = lax.axis_index("sp")
    sp_count = lax.axis_size("sp")
    scaling = HEAD ** (-0.5)
    q_float, q_inverse, q_normed = normalize(queries[0], gain_q_full)
    k_normed = (k_float * k_inverse * gain_k_full).astype(jnp.bfloat16)
    output_local = grad_output[0]
    query_heads = q_normed.reshape(tok_rows, HEADS, HEAD)
    output_heads = output_local.reshape(tok_rows, HEADS, HEAD)
    own_pos = jnp.arange(tok_rows, dtype=jnp.int32)
    own_time, own_col = tile_place(own_pos)
    own_row = jnp.zeros((tok_rows,), jnp.int32) + my_index
    ext_pos = jnp.arange(3 * tok_rows, dtype=jnp.int32)
    ext_time, ext_col = tile_place(ext_pos % tok_rows)
    ext_row = my_index - 1 + ext_pos // tok_rows
    ext_valid = (ext_row >= 0) & (ext_row < sp_count)
    masks = (own_time, own_col, own_row, ext_time, ext_col, ext_row, ext_valid)
    middle = slice(tok_rows, 2 * tok_rows)
    results, received, near_dg = [], [], []
    for c in range(chunks):
        if c > 0:
            extended[c], held = lax.optimization_barrier((extended[c], sent))
        cols = slice(bounds[c] * HEAD, bounds[c + 1] * HEAD)
        heads = slice(bounds[c], bounds[c + 1])
        chunk_heads = bounds[c + 1] - bounds[c]
        lo_float = extended[c][0, :tok_rows].astype(jnp.float32)
        hi_float = extended[c][0, 2 * tok_rows :].astype(jnp.float32)
        gain_c = gain_k_full[cols]
        key_ext = jnp.concatenate([
            (lo_float * lo_inverse * gain_c).astype(jnp.bfloat16),
            k_normed[:, cols],
            (hi_float * hi_inverse * gain_c).astype(jnp.bfloat16),
        ]).reshape(3 * tok_rows, chunk_heads, HEAD)
        value_ext = extended[c][1].reshape(3 * tok_rows, chunk_heads, HEAD)
        mixed_c, dq_c, dk_c, dv_c = attend_chunk(
            query_heads[:, heads], output_heads[:, heads], key_ext, value_ext,
            windows[heads], masks, scaling, group_size,
        )
        lower_send = jnp.stack([dk_c[:tok_rows], dv_c[:tok_rows]]).astype(jnp.bfloat16)
        upper_send = jnp.stack([dk_c[2 * tok_rows :], dv_c[2 * tok_rows :]]).astype(jnp.bfloat16)
        received.append((passed_along(lower_send, "sp", -1), passed_along(upper_send, "sp", 1)))
        sent = (lower_send, upper_send)
        results.append((mixed_c, dq_c, dk_c[middle], dv_c[middle]))
        near_dg.append(
            jnp.sum(lower_send[0].astype(jnp.float32) * lo_float * lo_inverse, axis=0)
            + jnp.sum(upper_send[0].astype(jnp.float32) * hi_float * hi_inverse, axis=0)
        )
    mixed_all = jnp.concatenate([r[0] for r in results], axis=1)
    dq_normed = jnp.concatenate([r[1] for r in results], axis=1)
    dk_own = jnp.concatenate([r[2] for r in results], axis=1)
    dv_own = jnp.concatenate([r[3] for r in results], axis=1)
    dq_out, dg_query = normalize_back(q_float, q_inverse, gain_q_full, dq_normed)
    dg_key = jnp.sum(dk_own * k_float * k_inverse, axis=0) + jnp.concatenate(near_dg)
    all_tokens = tok_rows * sp_count * lax.axis_size("clip") * lax.axis_size("fsdp")
    factor = all_tokens ** (-0.5)
    sizes = {axis: lax.axis_size(axis) for axis in ("fsdp", "clip", "sp")}
    partial_sums = jnp.stack([dg_query, dg_key])
    if all(count & (count - 1) == 0 for count in sizes.values()):
        steps = bits_of([("fsdp", sizes["fsdp"])])
        steps += [("sp", bit) for _, bit in bits_of([("sp", sizes["sp"])]) if bit > 1]
        steps += bits_of([("clip", sizes["clip"])]) + [("sp", 1)] * (sizes["sp"] > 1)
        totals = butterfly_sum(partial_sums, steps)
    else:
        totals = lax.psum(partial_sums, ("fsdp", "clip", "sp"))
    received, totals = lax.optimization_barrier((received, totals))
    lower = jnp.concatenate([r[0] for r in received], axis=2).astype(jnp.float32)
    upper = jnp.concatenate([r[1] for r in received], axis=2).astype(jnp.float32)
    dk_normed = dk_own + lower[0] + upper[0]
    dv_total = dv_own + lower[1] + upper[1]
    dk_out, _ = normalize_back(k_float, k_inverse, gain_k_full, dk_normed)
    share = gain_query.shape[0]
    totals = lax.dynamic_slice_in_dim(totals, lax.axis_index("fsdp") * share, share, axis=1)
    return (
        mixed_all.astype(jnp.bfloat16)[None],
        dq_out[None],
        dk_out[None],
        dv_total.astype(jnp.bfloat16)[None],
        totals[0] * factor,
        totals[1] * factor,
    )


def solution(mesh):
    return jax.shard_map(
        shards,
        mesh=mesh,
        in_specs=(
            P(("clip", "fsdp"), "sp", None),
            P(("clip", "fsdp"), "sp", None),
            P(("clip", "fsdp"), "sp", None),
            P(),
            P("fsdp"),
            P("fsdp"),
            P(("clip", "fsdp"), "sp", None),
        ),
        out_specs=(
            P(("clip", "fsdp"), "sp", None),
            P(("clip", "fsdp"), "sp", None),
            P(("clip", "fsdp"), "sp", None),
            P(("clip", "fsdp"), "sp", None),
            P("fsdp"),
            P("fsdp"),
        ),
        check_vma=False,
    )
```

```python
import jax
import jax.numpy as jnp
from jax import lax
from jax.sharding import PartitionSpec as P

HEADS = 20
HEAD = 128
TILE = 64
GW = 1


EPSILON = 1e-06
NEG_FILL = -1e30


def padded(block, sides, width):
    for axis, dim in sides:
        count = lax.axis_size(axis)
        forward = [(i, i + 1) for i in range(count - 1)]
        backward = [(target, source) for source, target in forward]
        low = lax.ppermute(
            lax.slice_in_dim(block, block.shape[dim] - width, None, axis=dim), axis, forward
        )
        high = lax.ppermute(lax.slice_in_dim(block, 0, width, axis=dim), axis, backward)
        block = jnp.concatenate([low, block, high], axis=dim)
    return block


def butterfly_gather(block, axis):
    count = lax.axis_size(axis)
    if count & (count - 1):
        return lax.all_gather(block, axis, axis=block.ndim - 1, tiled=True)
    me = lax.axis_index(axis)
    step = 1
    while step < count:
        other = lax.ppermute(block, axis, [(i, i ^ step) for i in range(count)])
        low_first = (me // step) % 2 == 0
        block = jnp.where(
            low_first,
            jnp.concatenate([block, other], axis=-1),
            jnp.concatenate([other, block], axis=-1),
        )
        step *= 2
    return block


def butterfly_sum(total, steps):
    for axis, bit in steps:
        count = lax.axis_size(axis)
        total = total + lax.ppermute(total, axis, [(i, i ^ bit) for i in range(count)])
    return total


def bits_of(axis_sizes):
    steps = []
    for axis, count in axis_sizes:
        bit = 1
        while bit < count:
            steps.append((axis, bit))
            bit *= 2
    return steps


def halving_scatter(total, axis):
    count = lax.axis_size(axis)
    me = lax.axis_index(axis)
    rows = total.shape[0]
    total = total.reshape(rows, count, -1)
    bit = count // 2
    while bit >= 1:
        split = total.reshape(rows, -1, 2, bit, total.shape[-1])
        high = (me // bit) % 2 == 1
        keep = jnp.where(high, split[:, :, 1], split[:, :, 0])
        give = jnp.where(high, split[:, :, 0], split[:, :, 1])
        total = keep + lax.ppermute(give, axis, [(i, i ^ bit) for i in range(count)])
        total = total.reshape(rows, -1, total.shape[-1])
        bit //= 2
    return total.reshape(rows, -1)


def passed_along(block, axis, distance):
    devices = range(lax.axis_size(axis))
    route = [(i - distance, i) for i in devices if i - distance in devices]
    return lax.ppermute(block, axis, route)


def product(pattern, left_side, right_side):
    return jnp.einsum(pattern, left_side, right_side, preferred_element_type=jnp.float32)


def tile_place(position):
    tile_number = position // TILE
    return (tile_number // GW, tile_number % GW)


def window_mask(radius, query_time, query_col, query_row, key_time, key_col, key_row, key_valid):
    apart_time = jnp.abs(query_time[:, None] - key_time[None, :])
    apart_col = jnp.abs(query_col[:, None] - key_col[None, :])
    apart_row = jnp.abs(query_row[:, None] - key_row[None, :])
    inside = apart_time[None] <= radius[:, 0, None, None]
    inside = inside & (apart_row[None] <= radius[:, 1, None, None])
    inside = inside & (apart_col[None] <= radius[:, 2, None, None])
    return inside & key_valid[None, None, :]


def normalize(raw_rows, gain_full):
    as_float = raw_rows.astype(jnp.float32)
    inverse = lax.rsqrt(jnp.mean(as_float * as_float, axis=-1, keepdims=True) + EPSILON)
    return (as_float, inverse, (as_float * inverse * gain_full).astype(jnp.bfloat16))


def normalize_back(as_float, inverse, gain_full, d_normed):
    scaled = gain_full * d_normed
    inner = jnp.mean(scaled * as_float, axis=-1, keepdims=True)
    d_raw = inverse * scaled - as_float * (inverse * inverse * inverse) * inner
    return (d_raw.astype(jnp.bfloat16), jnp.sum(d_normed * as_float * inverse, axis=0))


def forward_group(query_part, key_part, value_part, allowed, scaling):
    scores = product("qhd,khd->hqk", query_part, key_part) * scaling
    scores = jnp.where(allowed, scores, NEG_FILL)
    row_max = jnp.max(scores, axis=2, keepdims=True)
    row_sum = jnp.sum(jnp.exp(scores - row_max), axis=2, keepdims=True)
    log_sum = row_max + jnp.log(row_sum)
    weights = jnp.exp(scores - log_sum)
    weights_low = weights.astype(jnp.bfloat16)
    mixed = product("hqk,khd->qhd", weights_low, value_part)
    return (weights, weights_low, mixed, log_sum[:, :, 0])


def score_grads(weights, output_part, value_part, delta, scaling):
    d_weights = product("qhd,khd->hqk", output_part, value_part)
    return (weights * (d_weights - delta[:, :, None]) * scaling).astype(jnp.bfloat16)


def attend_chunk(query_heads, output_heads, key_ext, value_ext, windows, masks, scaling, group_size):
    own_time, own_col, own_row, ext_time, ext_col, ext_row, ext_valid = masks
    heads = query_heads.shape[1]
    mixed_parts, dq_parts, dk_parts, dv_parts = ([], [], [], [])
    for first_head in range(0, heads, group_size):
        head_range = slice(first_head, first_head + group_size)
        allowed = window_mask(
            windows[head_range], own_time, own_col, own_row, ext_time, ext_col, ext_row, ext_valid
        )
        weights, weights_low, mixed, log_sum = forward_group(
            query_heads[:, head_range],
            key_ext[:, head_range],
            value_ext[:, head_range],
            allowed,
            scaling,
        )
        delta = jnp.sum(output_heads[:, head_range] * mixed, axis=2).T
        d_scores = score_grads(
            weights, output_heads[:, head_range], value_ext[:, head_range], delta, scaling
        )
        dq_parts.append(product("hqk,khd->qhd", d_scores, key_ext[:, head_range]))
        dk_parts.append(product("hqk,qhd->khd", d_scores, query_heads[:, head_range]))
        dv_parts.append(product("hqk,qhd->khd", weights_low, output_heads[:, head_range]))
        mixed_parts.append(mixed)
    rows = query_heads.shape[0]
    width = heads * HEAD
    return (
        jnp.concatenate(mixed_parts, axis=1).reshape(rows, width),
        jnp.concatenate(dq_parts, axis=1).reshape(rows, width),
        jnp.concatenate(dk_parts, axis=1).reshape(-1, width),
        jnp.concatenate(dv_parts, axis=1).reshape(-1, width),
    )


def shards(queries, key_vectors, value_vectors, windows, gain_query, gain_key, grad_output):
    tok_rows = queries.shape[1]
    width = HEADS * HEAD
    bounds = (0, 8, HEADS) if HEADS == 20 else (0, HEADS)
    chunks = len(bounds) - 1
    group_size = 4
    key_raw = key_vectors[0]
    value_local = value_vectors[0]
    extended = [
        padded(
            jnp.stack([key_raw[:, bounds[c] * HEAD : bounds[c + 1] * HEAD],
                       value_local[:, bounds[c] * HEAD : bounds[c + 1] * HEAD]]),
            (("sp", 1),),
            tok_rows,
        )
        for c in range(chunks)
    ]
    k_float = key_raw.astype(jnp.float32)
    k_inverse = lax.rsqrt(jnp.mean(k_float * k_float, axis=-1, keepdims=True) + EPSILON)
    inverse_ext = padded(k_inverse, (("sp", 0),), tok_rows)
    lo_inverse, hi_inverse = inverse_ext[:tok_rows], inverse_ext[2 * tok_rows :]
    gains = butterfly_gather(jnp.stack([gain_query, gain_key]), "fsdp")
    gain_q_full, gain_k_full = gains[0], gains[1]
    my_index = lax.axis_index("sp")
    sp_count = lax.axis_size("sp")
    scaling = HEAD ** (-0.5)
    q_float, q_inverse, q_normed = normalize(queries[0], gain_q_full)
    k_normed = (k_float * k_inverse * gain_k_full).astype(jnp.bfloat16)
    output_local = grad_output[0]
    query_heads = q_normed.reshape(tok_rows, HEADS, HEAD)
    output_heads = output_local.reshape(tok_rows, HEADS, HEAD)
    own_pos = jnp.arange(tok_rows, dtype=jnp.int32)
    own_time, own_col = tile_place(own_pos)
    own_row = jnp.zeros((tok_rows,), jnp.int32) + my_index
    ext_pos = jnp.arange(3 * tok_rows, dtype=jnp.int32)
    ext_time, ext_col = tile_place(ext_pos % tok_rows)
    ext_row = my_index - 1 + ext_pos // tok_rows
    ext_valid = (ext_row >= 0) & (ext_row < sp_count)
    masks = (own_time, own_col, own_row, ext_time, ext_col, ext_row, ext_valid)
    middle = slice(tok_rows, 2 * tok_rows)
    results, received, near_dg = [], [], []
    for c in range(chunks):
        if c > 0:
            extended[c], held = lax.optimization_barrier((extended[c], sent))
        cols = slice(bounds[c] * HEAD, bounds[c + 1] * HEAD)
        heads = slice(bounds[c], bounds[c + 1])
        chunk_heads = bounds[c + 1] - bounds[c]
        lo_float = extended[c][0, :tok_rows].astype(jnp.float32)
        hi_float = extended[c][0, 2 * tok_rows :].astype(jnp.float32)
        gain_c = gain_k_full[cols]
        key_ext = jnp.concatenate([
            (lo_float * lo_inverse * gain_c).astype(jnp.bfloat16),
            k_normed[:, cols],
            (hi_float * hi_inverse * gain_c).astype(jnp.bfloat16),
        ]).reshape(3 * tok_rows, chunk_heads, HEAD)
        value_ext = extended[c][1].reshape(3 * tok_rows, chunk_heads, HEAD)
        mixed_c, dq_c, dk_c, dv_c = attend_chunk(
            query_heads[:, heads], output_heads[:, heads], key_ext, value_ext,
            windows[heads], masks, scaling, group_size,
        )
        lower_send = jnp.stack([dk_c[:tok_rows], dv_c[:tok_rows]]).astype(jnp.bfloat16)
        upper_send = jnp.stack([dk_c[2 * tok_rows :], dv_c[2 * tok_rows :]]).astype(jnp.bfloat16)
        received.append((passed_along(lower_send, "sp", -1), passed_along(upper_send, "sp", 1)))
        sent = (lower_send, upper_send)
        results.append((mixed_c, dq_c, dk_c[middle], dv_c[middle]))
        near_dg.append(
            jnp.sum(lower_send[0].astype(jnp.float32) * lo_float * lo_inverse, axis=0)
            + jnp.sum(upper_send[0].astype(jnp.float32) * hi_float * hi_inverse, axis=0)
        )
    mixed_all = jnp.concatenate([r[0] for r in results], axis=1)
    dq_normed = jnp.concatenate([r[1] for r in results], axis=1)
    dk_own = jnp.concatenate([r[2] for r in results], axis=1)
    dv_own = jnp.concatenate([r[3] for r in results], axis=1)
    dq_out, dg_query = normalize_back(q_float, q_inverse, gain_q_full, dq_normed)
    dg_key = jnp.sum(dk_own * k_float * k_inverse, axis=0) + jnp.concatenate(near_dg)
    all_tokens = tok_rows * sp_count * lax.axis_size("clip") * lax.axis_size("fsdp")
    factor = all_tokens ** (-0.5)
    sizes = {axis: lax.axis_size(axis) for axis in ("fsdp", "clip", "sp")}
    partial_sums = jnp.stack([dg_query, dg_key])
    share = gain_query.shape[0]
    if all(count & (count - 1) == 0 for count in sizes.values()):
        totals = halving_scatter(partial_sums, "fsdp")
        totals = butterfly_sum(
            totals, [("sp", bit) for _, bit in bits_of([("sp", sizes["sp"])]) if bit > 1]
        )
        received, totals = lax.optimization_barrier((received, totals))
        totals = butterfly_sum(
            totals, bits_of([("clip", sizes["clip"])]) + [("sp", 1)] * (sizes["sp"] > 1)
        )
    else:
        totals = lax.psum(partial_sums, ("fsdp", "clip", "sp"))
        received, totals = lax.optimization_barrier((received, totals))
        totals = lax.dynamic_slice_in_dim(totals, lax.axis_index("fsdp") * share, share, axis=1)
    lower = jnp.concatenate([r[0] for r in received], axis=2).astype(jnp.float32)
    upper = jnp.concatenate([r[1] for r in received], axis=2).astype(jnp.float32)
    dk_normed = dk_own + lower[0] + upper[0]
    dv_total = dv_own + lower[1] + upper[1]
    dk_out, _ = normalize_back(k_float, k_inverse, gain_k_full, dk_normed)
    return (
        mixed_all.astype(jnp.bfloat16)[None],
        dq_out[None],
        dk_out[None],
        dv_total.astype(jnp.bfloat16)[None],
        totals[0] * factor,
        totals[1] * factor,
    )


def solution(mesh):
    return jax.shard_map(
        shards,
        mesh=mesh,
        in_specs=(
            P(("clip", "fsdp"), "sp", None),
            P(("clip", "fsdp"), "sp", None),
            P(("clip", "fsdp"), "sp", None),
            P(),
            P("fsdp"),
            P("fsdp"),
            P(("clip", "fsdp"), "sp", None),
        ),
        out_specs=(
            P(("clip", "fsdp"), "sp", None),
            P(("clip", "fsdp"), "sp", None),
            P(("clip", "fsdp"), "sp", None),
            P(("clip", "fsdp"), "sp", None),
            P("fsdp"),
            P("fsdp"),
        ),
        check_vma=False,
    )
```

```python
import jax
import jax.numpy as jnp
from jax import lax
from jax.sharding import PartitionSpec as P

HEADS = 20
HEAD = 128
TILE = 64
GW = 1


EPSILON = 1e-06
NEG_FILL = -1e30


def padded(block, sides, width):
    for axis, dim in sides:
        count = lax.axis_size(axis)
        forward = [(i, i + 1) for i in range(count - 1)]
        backward = [(target, source) for source, target in forward]
        low = lax.ppermute(
            lax.slice_in_dim(block, block.shape[dim] - width, None, axis=dim), axis, forward
        )
        high = lax.ppermute(lax.slice_in_dim(block, 0, width, axis=dim), axis, backward)
        block = jnp.concatenate([low, block, high], axis=dim)
    return block


def butterfly_gather(block, axis):
    count = lax.axis_size(axis)
    if count & (count - 1):
        return lax.all_gather(block, axis, axis=block.ndim - 1, tiled=True)
    me = lax.axis_index(axis)
    step = 1
    while step < count:
        other = lax.ppermute(block, axis, [(i, i ^ step) for i in range(count)])
        low_first = (me // step) % 2 == 0
        block = jnp.where(
            low_first,
            jnp.concatenate([block, other], axis=-1),
            jnp.concatenate([other, block], axis=-1),
        )
        step *= 2
    return block


def butterfly_sum(total, steps):
    for axis, bit in steps:
        count = lax.axis_size(axis)
        total = total + lax.ppermute(total, axis, [(i, i ^ bit) for i in range(count)])
    return total


def bits_of(axis_sizes):
    steps = []
    for axis, count in axis_sizes:
        bit = 1
        while bit < count:
            steps.append((axis, bit))
            bit *= 2
    return steps


def passed_along(block, axis, distance):
    devices = range(lax.axis_size(axis))
    route = [(i - distance, i) for i in devices if i - distance in devices]
    return lax.ppermute(block, axis, route)


def product(pattern, left_side, right_side):
    return jnp.einsum(pattern, left_side, right_side, preferred_element_type=jnp.float32)


def tile_place(position):
    tile_number = position // TILE
    return (tile_number // GW, tile_number % GW)


def window_mask(radius, query_time, query_col, query_row, key_time, key_col, key_row, key_valid):
    apart_time = jnp.abs(query_time[:, None] - key_time[None, :])
    apart_col = jnp.abs(query_col[:, None] - key_col[None, :])
    apart_row = jnp.abs(query_row[:, None] - key_row[None, :])
    inside = apart_time[None] <= radius[:, 0, None, None]
    inside = inside & (apart_row[None] <= radius[:, 1, None, None])
    inside = inside & (apart_col[None] <= radius[:, 2, None, None])
    return inside & key_valid[None, None, :]


def normalize(raw_rows, gain_full):
    as_float = raw_rows.astype(jnp.float32)
    inverse = lax.rsqrt(jnp.mean(as_float * as_float, axis=-1, keepdims=True) + EPSILON)
    return (as_float, inverse, (as_float * inverse * gain_full).astype(jnp.bfloat16))


def normalize_back(as_float, inverse, gain_full, d_normed):
    scaled = gain_full * d_normed
    inner = jnp.mean(scaled * as_float, axis=-1, keepdims=True)
    d_raw = inverse * scaled - as_float * (inverse * inverse * inverse) * inner
    return (d_raw.astype(jnp.bfloat16), jnp.sum(d_normed * as_float * inverse, axis=0))


def forward_group(query_part, key_part, value_part, allowed, scaling):
    scores = product("qhd,khd->hqk", query_part, key_part) * scaling
    scores = jnp.where(allowed, scores, NEG_FILL)
    row_max = jnp.max(scores, axis=2, keepdims=True)
    row_sum = jnp.sum(jnp.exp(scores - row_max), axis=2, keepdims=True)
    log_sum = row_max + jnp.log(row_sum)
    weights = jnp.exp(scores - log_sum)
    weights_low = weights.astype(jnp.bfloat16)
    mixed = product("hqk,khd->qhd", weights_low, value_part)
    return (weights, weights_low, mixed, log_sum[:, :, 0])


def score_grads(weights, output_part, value_part, delta, scaling):
    d_weights = product("qhd,khd->hqk", output_part, value_part)
    return (weights * (d_weights - delta[:, :, None]) * scaling).astype(jnp.bfloat16)


def attend_chunk(query_heads, output_heads, key_ext, value_ext, windows, masks, scaling, group_size):
    own_time, own_col, own_row, ext_time, ext_col, ext_row, ext_valid = masks
    heads = query_heads.shape[1]
    mixed_parts, dq_parts, dk_parts, dv_parts = ([], [], [], [])
    for first_head in range(0, heads, group_size):
        head_range = slice(first_head, first_head + group_size)
        allowed = window_mask(
            windows[head_range], own_time, own_col, own_row, ext_time, ext_col, ext_row, ext_valid
        )
        weights, weights_low, mixed, log_sum = forward_group(
            query_heads[:, head_range],
            key_ext[:, head_range],
            value_ext[:, head_range],
            allowed,
            scaling,
        )
        delta = jnp.sum(output_heads[:, head_range] * mixed, axis=2).T
        d_scores = score_grads(
            weights, output_heads[:, head_range], value_ext[:, head_range], delta, scaling
        )
        dq_parts.append(product("hqk,khd->qhd", d_scores, key_ext[:, head_range]))
        dk_parts.append(product("hqk,qhd->khd", d_scores, query_heads[:, head_range]))
        dv_parts.append(product("hqk,qhd->khd", weights_low, output_heads[:, head_range]))
        mixed_parts.append(mixed)
    rows = query_heads.shape[0]
    width = heads * HEAD
    return (
        jnp.concatenate(mixed_parts, axis=1).reshape(rows, width),
        jnp.concatenate(dq_parts, axis=1).reshape(rows, width),
        jnp.concatenate(dk_parts, axis=1).reshape(-1, width),
        jnp.concatenate(dv_parts, axis=1).reshape(-1, width),
    )


def shards(queries, key_vectors, value_vectors, windows, gain_query, gain_key, grad_output):
    tok_rows = queries.shape[1]
    width = HEADS * HEAD
    bounds = (0, 8, HEADS) if HEADS == 20 else (0, HEADS)
    chunks = len(bounds) - 1
    group_size = 4
    key_raw = key_vectors[0]
    value_local = value_vectors[0]
    extended = [
        padded(
            jnp.stack([key_raw[:, bounds[c] * HEAD : bounds[c + 1] * HEAD],
                       value_local[:, bounds[c] * HEAD : bounds[c + 1] * HEAD]]),
            (("sp", 1),),
            tok_rows,
        )
        for c in range(chunks)
    ]
    k_float = key_raw.astype(jnp.float32)
    k_inverse = lax.rsqrt(jnp.mean(k_float * k_float, axis=-1, keepdims=True) + EPSILON)
    inverse_ext = padded(k_inverse, (("sp", 0),), tok_rows)
    lo_inverse, hi_inverse = inverse_ext[:tok_rows], inverse_ext[2 * tok_rows :]
    gains = butterfly_gather(jnp.stack([gain_query, gain_key]), "fsdp")
    gain_q_full, gain_k_full = gains[0], gains[1]
    my_index = lax.axis_index("sp")
    sp_count = lax.axis_size("sp")
    scaling = HEAD ** (-0.5)
    q_float, q_inverse, q_normed = normalize(queries[0], gain_q_full)
    k_normed = (k_float * k_inverse * gain_k_full).astype(jnp.bfloat16)
    output_local = grad_output[0]
    query_heads = q_normed.reshape(tok_rows, HEADS, HEAD)
    output_heads = output_local.reshape(tok_rows, HEADS, HEAD)
    own_pos = jnp.arange(tok_rows, dtype=jnp.int32)
    own_time, own_col = tile_place(own_pos)
    own_row = jnp.zeros((tok_rows,), jnp.int32) + my_index
    ext_pos = jnp.arange(3 * tok_rows, dtype=jnp.int32)
    ext_time, ext_col = tile_place(ext_pos % tok_rows)
    ext_row = my_index - 1 + ext_pos // tok_rows
    ext_valid = (ext_row >= 0) & (ext_row < sp_count)
    masks = (own_time, own_col, own_row, ext_time, ext_col, ext_row, ext_valid)
    middle = slice(tok_rows, 2 * tok_rows)
    results, received, near_dg = [], [], []
    for c in range(chunks):
        if c > 0:
            extended[c], held = lax.optimization_barrier((extended[c], sent))
        cols = slice(bounds[c] * HEAD, bounds[c + 1] * HEAD)
        heads = slice(bounds[c], bounds[c + 1])
        chunk_heads = bounds[c + 1] - bounds[c]
        lo_float = extended[c][0, :tok_rows].astype(jnp.float32)
        hi_float = extended[c][0, 2 * tok_rows :].astype(jnp.float32)
        gain_c = gain_k_full[cols]
        key_ext = jnp.concatenate([
            (lo_float * lo_inverse * gain_c).astype(jnp.bfloat16),
            k_normed[:, cols],
            (hi_float * hi_inverse * gain_c).astype(jnp.bfloat16),
        ]).reshape(3 * tok_rows, chunk_heads, HEAD)
        value_ext = extended[c][1].reshape(3 * tok_rows, chunk_heads, HEAD)
        mixed_c, dq_c, dk_c, dv_c = attend_chunk(
            query_heads[:, heads], output_heads[:, heads], key_ext, value_ext,
            windows[heads], masks, scaling, group_size,
        )
        lower_send = jnp.stack([dk_c[:tok_rows], dv_c[:tok_rows]]).astype(jnp.bfloat16)
        upper_send = jnp.stack([dk_c[2 * tok_rows :], dv_c[2 * tok_rows :]]).astype(jnp.bfloat16)
        received.append((passed_along(lower_send, "sp", -1), passed_along(upper_send, "sp", 1)))
        sent = (lower_send, upper_send)
        results.append((mixed_c, dq_c, dk_c[middle], dv_c[middle]))
        near_dg.append(
            jnp.sum(lower_send[0].astype(jnp.float32) * lo_float * lo_inverse, axis=0)
            + jnp.sum(upper_send[0].astype(jnp.float32) * hi_float * hi_inverse, axis=0)
        )
    mixed_all = jnp.concatenate([r[0] for r in results], axis=1)
    dq_normed = jnp.concatenate([r[1] for r in results], axis=1)
    dk_own = jnp.concatenate([r[2] for r in results], axis=1)
    dv_own = jnp.concatenate([r[3] for r in results], axis=1)
    dq_out, dg_query = normalize_back(q_float, q_inverse, gain_q_full, dq_normed)
    dg_key = jnp.sum(dk_own * k_float * k_inverse, axis=0) + jnp.concatenate(near_dg)
    all_tokens = tok_rows * sp_count * lax.axis_size("clip") * lax.axis_size("fsdp")
    factor = all_tokens ** (-0.5)
    sizes = {axis: lax.axis_size(axis) for axis in ("fsdp", "clip", "sp")}
    partial_sums = jnp.stack([dg_query, dg_key])
    if all(count & (count - 1) == 0 for count in sizes.values()):
        steps = bits_of([("fsdp", sizes["fsdp"])])
        steps += [("sp", bit) for _, bit in bits_of([("sp", sizes["sp"])]) if bit > 1]
        totals = butterfly_sum(partial_sums, steps)
        received, totals = lax.optimization_barrier((received, totals))
        totals = butterfly_sum(
            totals, bits_of([("clip", sizes["clip"])]) + [("sp", 1)] * (sizes["sp"] > 1)
        )
    else:
        totals = lax.psum(partial_sums, ("fsdp", "clip", "sp"))
        received, totals = lax.optimization_barrier((received, totals))
    lower = jnp.concatenate([r[0] for r in received], axis=2).astype(jnp.float32)
    upper = jnp.concatenate([r[1] for r in received], axis=2).astype(jnp.float32)
    dk_normed = dk_own + lower[0] + upper[0]
    dv_total = dv_own + lower[1] + upper[1]
    dk_out, _ = normalize_back(k_float, k_inverse, gain_k_full, dk_normed)
    share = gain_query.shape[0]
    totals = lax.dynamic_slice_in_dim(totals, lax.axis_index("fsdp") * share, share, axis=1)
    return (
        mixed_all.astype(jnp.bfloat16)[None],
        dq_out[None],
        dk_out[None],
        dv_total.astype(jnp.bfloat16)[None],
        totals[0] * factor,
        totals[1] * factor,
    )


def solution(mesh):
    return jax.shard_map(
        shards,
        mesh=mesh,
        in_specs=(
            P(("clip", "fsdp"), "sp", None),
            P(("clip", "fsdp"), "sp", None),
            P(("clip", "fsdp"), "sp", None),
            P(),
            P("fsdp"),
            P("fsdp"),
            P(("clip", "fsdp"), "sp", None),
        ),
        out_specs=(
            P(("clip", "fsdp"), "sp", None),
            P(("clip", "fsdp"), "sp", None),
            P(("clip", "fsdp"), "sp", None),
            P(("clip", "fsdp"), "sp", None),
            P("fsdp"),
            P("fsdp"),
        ),
        check_vma=False,
    )
```

```python
import jax
import jax.numpy as jnp
from jax import lax
from jax.sharding import PartitionSpec as P

HEADS = 20
HEAD = 128
TILE = 64
GW = 1


EPSILON = 1e-06
NEG_FILL = -1e30


def padded(block, sides, width):
    for axis, dim in sides:
        count = lax.axis_size(axis)
        forward = [(i, i + 1) for i in range(count - 1)]
        backward = [(target, source) for source, target in forward]
        low = lax.ppermute(
            lax.slice_in_dim(block, block.shape[dim] - width, None, axis=dim), axis, forward
        )
        high = lax.ppermute(lax.slice_in_dim(block, 0, width, axis=dim), axis, backward)
        block = jnp.concatenate([low, block, high], axis=dim)
    return block


def butterfly_gather(block, axis):
    count = lax.axis_size(axis)
    if count & (count - 1):
        return lax.all_gather(block, axis, axis=block.ndim - 1, tiled=True)
    me = lax.axis_index(axis)
    step = 1
    while step < count:
        other = lax.ppermute(block, axis, [(i, i ^ step) for i in range(count)])
        low_first = (me // step) % 2 == 0
        block = jnp.where(
            low_first,
            jnp.concatenate([block, other], axis=-1),
            jnp.concatenate([other, block], axis=-1),
        )
        step *= 2
    return block


def butterfly_sum(total, steps):
    for axis, bit in steps:
        count = lax.axis_size(axis)
        total = total + lax.ppermute(total, axis, [(i, i ^ bit) for i in range(count)])
    return total


def bits_of(axis_sizes):
    steps = []
    for axis, count in axis_sizes:
        bit = 1
        while bit < count:
            steps.append((axis, bit))
            bit *= 2
    return steps


def passed_along(block, axis, distance):
    devices = range(lax.axis_size(axis))
    route = [(i - distance, i) for i in devices if i - distance in devices]
    return lax.ppermute(block, axis, route)


def product(pattern, left_side, right_side):
    return jnp.einsum(pattern, left_side, right_side, preferred_element_type=jnp.float32)


def tile_place(position):
    tile_number = position // TILE
    return (tile_number // GW, tile_number % GW)


def window_mask(radius, query_time, query_col, query_row, key_time, key_col, key_row, key_valid):
    apart_time = jnp.abs(query_time[:, None] - key_time[None, :])
    apart_col = jnp.abs(query_col[:, None] - key_col[None, :])
    apart_row = jnp.abs(query_row[:, None] - key_row[None, :])
    inside = apart_time[None] <= radius[:, 0, None, None]
    inside = inside & (apart_row[None] <= radius[:, 1, None, None])
    inside = inside & (apart_col[None] <= radius[:, 2, None, None])
    return inside & key_valid[None, None, :]


def normalize(raw_rows, gain_full):
    as_float = raw_rows.astype(jnp.float32)
    inverse = lax.rsqrt(jnp.mean(as_float * as_float, axis=-1, keepdims=True) + EPSILON)
    return (as_float, inverse, (as_float * inverse * gain_full).astype(jnp.bfloat16))


def normalize_back(as_float, inverse, gain_full, d_normed):
    scaled = gain_full * d_normed
    inner = jnp.mean(scaled * as_float, axis=-1, keepdims=True)
    d_raw = inverse * scaled - as_float * (inverse * inverse * inverse) * inner
    return (d_raw.astype(jnp.bfloat16), jnp.sum(d_normed * as_float * inverse, axis=0))


def forward_group(query_part, key_part, value_part, allowed, scaling):
    scores = product("qhd,khd->hqk", query_part, key_part) * scaling
    scores = jnp.where(allowed, scores, NEG_FILL)
    row_max = jnp.max(scores, axis=2, keepdims=True)
    row_sum = jnp.sum(jnp.exp(scores - row_max), axis=2, keepdims=True)
    log_sum = row_max + jnp.log(row_sum)
    weights = jnp.exp(scores - log_sum)
    weights_low = weights.astype(jnp.bfloat16)
    mixed = product("hqk,khd->qhd", weights_low, value_part)
    return (weights, weights_low, mixed, log_sum[:, :, 0])


def score_grads(weights, output_part, value_part, delta, scaling):
    d_weights = product("qhd,khd->hqk", output_part, value_part)
    return (weights * (d_weights - delta[:, :, None]) * scaling).astype(jnp.bfloat16)


def attend_chunk(query_heads, output_heads, key_ext, value_ext, windows, masks, scaling, group_size):
    own_time, own_col, own_row, ext_time, ext_col, ext_row, ext_valid = masks
    heads = query_heads.shape[1]
    mixed_parts, dq_parts, dk_parts, dv_parts = ([], [], [], [])
    for first_head in range(0, heads, group_size):
        head_range = slice(first_head, first_head + group_size)
        allowed = window_mask(
            windows[head_range], own_time, own_col, own_row, ext_time, ext_col, ext_row, ext_valid
        )
        weights, weights_low, mixed, log_sum = forward_group(
            query_heads[:, head_range],
            key_ext[:, head_range],
            value_ext[:, head_range],
            allowed,
            scaling,
        )
        delta = jnp.sum(output_heads[:, head_range] * mixed, axis=2).T
        d_scores = score_grads(
            weights, output_heads[:, head_range], value_ext[:, head_range], delta, scaling
        )
        dq_parts.append(product("hqk,khd->qhd", d_scores, key_ext[:, head_range]))
        dk_parts.append(product("hqk,qhd->khd", d_scores, query_heads[:, head_range]))
        dv_parts.append(product("hqk,qhd->khd", weights_low, output_heads[:, head_range]))
        mixed_parts.append(mixed)
    rows = query_heads.shape[0]
    width = heads * HEAD
    return (
        jnp.concatenate(mixed_parts, axis=1).reshape(rows, width),
        jnp.concatenate(dq_parts, axis=1).reshape(rows, width),
        jnp.concatenate(dk_parts, axis=1).reshape(-1, width),
        jnp.concatenate(dv_parts, axis=1).reshape(-1, width),
    )


def shards(queries, key_vectors, value_vectors, windows, gain_query, gain_key, grad_output):
    tok_rows = queries.shape[1]
    width = HEADS * HEAD
    bounds = (0, 8, HEADS) if HEADS == 20 else (0, HEADS)
    chunks = len(bounds) - 1
    group_size = 4
    key_raw = key_vectors[0]
    value_local = value_vectors[0]
    extended = [
        padded(
            jnp.stack([key_raw[:, bounds[c] * HEAD : bounds[c + 1] * HEAD],
                       value_local[:, bounds[c] * HEAD : bounds[c + 1] * HEAD]]),
            (("sp", 1),),
            tok_rows,
        )
        for c in range(chunks)
    ]
    k_float = key_raw.astype(jnp.float32)
    k_inverse = lax.rsqrt(jnp.mean(k_float * k_float, axis=-1, keepdims=True) + EPSILON)
    inverse_ext = padded(k_inverse, (("sp", 0),), tok_rows)
    lo_inverse, hi_inverse = inverse_ext[:tok_rows], inverse_ext[2 * tok_rows :]
    gains = lax.all_gather(jnp.stack([gain_query, gain_key]), "fsdp", axis=1, tiled=True)
    gain_q_full, gain_k_full = gains[0], gains[1]
    my_index = lax.axis_index("sp")
    sp_count = lax.axis_size("sp")
    scaling = HEAD ** (-0.5)
    q_float, q_inverse, q_normed = normalize(queries[0], gain_q_full)
    k_normed = (k_float * k_inverse * gain_k_full).astype(jnp.bfloat16)
    output_local = grad_output[0]
    query_heads = q_normed.reshape(tok_rows, HEADS, HEAD)
    output_heads = output_local.reshape(tok_rows, HEADS, HEAD)
    own_pos = jnp.arange(tok_rows, dtype=jnp.int32)
    own_time, own_col = tile_place(own_pos)
    own_row = jnp.zeros((tok_rows,), jnp.int32) + my_index
    ext_pos = jnp.arange(3 * tok_rows, dtype=jnp.int32)
    ext_time, ext_col = tile_place(ext_pos % tok_rows)
    ext_row = my_index - 1 + ext_pos // tok_rows
    ext_valid = (ext_row >= 0) & (ext_row < sp_count)
    masks = (own_time, own_col, own_row, ext_time, ext_col, ext_row, ext_valid)
    middle = slice(tok_rows, 2 * tok_rows)
    results, received, near_dg = [], [], []
    for c in range(chunks):
        if c > 0:
            extended[c], held = lax.optimization_barrier((extended[c], sent))
        cols = slice(bounds[c] * HEAD, bounds[c + 1] * HEAD)
        heads = slice(bounds[c], bounds[c + 1])
        chunk_heads = bounds[c + 1] - bounds[c]
        lo_float = extended[c][0, :tok_rows].astype(jnp.float32)
        hi_float = extended[c][0, 2 * tok_rows :].astype(jnp.float32)
        gain_c = gain_k_full[cols]
        key_ext = jnp.concatenate([
            (lo_float * lo_inverse * gain_c).astype(jnp.bfloat16),
            k_normed[:, cols],
            (hi_float * hi_inverse * gain_c).astype(jnp.bfloat16),
        ]).reshape(3 * tok_rows, chunk_heads, HEAD)
        value_ext = extended[c][1].reshape(3 * tok_rows, chunk_heads, HEAD)
        mixed_c, dq_c, dk_c, dv_c = attend_chunk(
            query_heads[:, heads], output_heads[:, heads], key_ext, value_ext,
            windows[heads], masks, scaling, group_size,
        )
        lower_send = jnp.stack([dk_c[:tok_rows], dv_c[:tok_rows]]).astype(jnp.bfloat16)
        upper_send = jnp.stack([dk_c[2 * tok_rows :], dv_c[2 * tok_rows :]]).astype(jnp.bfloat16)
        received.append((passed_along(lower_send, "sp", -1), passed_along(upper_send, "sp", 1)))
        sent = (lower_send, upper_send)
        results.append((mixed_c, dq_c, dk_c[middle], dv_c[middle]))
        near_dg.append(
            jnp.sum(lower_send[0].astype(jnp.float32) * lo_float * lo_inverse, axis=0)
            + jnp.sum(upper_send[0].astype(jnp.float32) * hi_float * hi_inverse, axis=0)
        )
    mixed_all = jnp.concatenate([r[0] for r in results], axis=1)
    dq_normed = jnp.concatenate([r[1] for r in results], axis=1)
    dk_own = jnp.concatenate([r[2] for r in results], axis=1)
    dv_own = jnp.concatenate([r[3] for r in results], axis=1)
    dq_out, dg_query = normalize_back(q_float, q_inverse, gain_q_full, dq_normed)
    dg_key = jnp.sum(dk_own * k_float * k_inverse, axis=0) + jnp.concatenate(near_dg)
    all_tokens = tok_rows * sp_count * lax.axis_size("clip") * lax.axis_size("fsdp")
    factor = all_tokens ** (-0.5)
    sizes = {axis: lax.axis_size(axis) for axis in ("fsdp", "clip", "sp")}
    partial_sums = jnp.stack([dg_query, dg_key])
    if all(count & (count - 1) == 0 for count in sizes.values()):
        steps = bits_of([("fsdp", sizes["fsdp"])])
        steps += [("sp", bit) for _, bit in bits_of([("sp", sizes["sp"])]) if bit > 1]
        totals = butterfly_sum(partial_sums, steps)
        received, totals = lax.optimization_barrier((received, totals))
        totals = butterfly_sum(
            totals, bits_of([("clip", sizes["clip"])]) + [("sp", 1)] * (sizes["sp"] > 1)
        )
    else:
        totals = lax.psum(partial_sums, ("fsdp", "clip", "sp"))
        received, totals = lax.optimization_barrier((received, totals))
    lower = jnp.concatenate([r[0] for r in received], axis=2).astype(jnp.float32)
    upper = jnp.concatenate([r[1] for r in received], axis=2).astype(jnp.float32)
    dk_normed = dk_own + lower[0] + upper[0]
    dv_total = dv_own + lower[1] + upper[1]
    dk_out, _ = normalize_back(k_float, k_inverse, gain_k_full, dk_normed)
    share = gain_query.shape[0]
    totals = lax.dynamic_slice_in_dim(totals, lax.axis_index("fsdp") * share, share, axis=1)
    return (
        mixed_all.astype(jnp.bfloat16)[None],
        dq_out[None],
        dk_out[None],
        dv_total.astype(jnp.bfloat16)[None],
        totals[0] * factor,
        totals[1] * factor,
    )


def solution(mesh):
    return jax.shard_map(
        shards,
        mesh=mesh,
        in_specs=(
            P(("clip", "fsdp"), "sp", None),
            P(("clip", "fsdp"), "sp", None),
            P(("clip", "fsdp"), "sp", None),
            P(),
            P("fsdp"),
            P("fsdp"),
            P(("clip", "fsdp"), "sp", None),
        ),
        out_specs=(
            P(("clip", "fsdp"), "sp", None),
            P(("clip", "fsdp"), "sp", None),
            P(("clip", "fsdp"), "sp", None),
            P(("clip", "fsdp"), "sp", None),
            P("fsdp"),
            P("fsdp"),
        ),
        check_vma=False,
    )
```

```python
import jax
import jax.numpy as jnp
from jax import lax
from jax.sharding import PartitionSpec as P

HEADS = 20
HEAD = 128
TILE = 64
GW = 1


EPSILON = 1e-06
NEG_FILL = -1e30


def padded(block, sides, width):
    for axis, dim in sides:
        count = lax.axis_size(axis)
        forward = [(i, i + 1) for i in range(count - 1)]
        backward = [(target, source) for source, target in forward]
        low = lax.ppermute(
            lax.slice_in_dim(block, block.shape[dim] - width, None, axis=dim), axis, forward
        )
        high = lax.ppermute(lax.slice_in_dim(block, 0, width, axis=dim), axis, backward)
        block = jnp.concatenate([low, block, high], axis=dim)
    return block


def butterfly_gather(block, axis):
    count = lax.axis_size(axis)
    if count & (count - 1):
        return lax.all_gather(block, axis, axis=block.ndim - 1, tiled=True)
    me = lax.axis_index(axis)
    step = 1
    while step < count:
        other = lax.ppermute(block, axis, [(i, i ^ step) for i in range(count)])
        low_first = (me // step) % 2 == 0
        block = jnp.where(
            low_first,
            jnp.concatenate([block, other], axis=-1),
            jnp.concatenate([other, block], axis=-1),
        )
        step *= 2
    return block


def butterfly_sum(total, steps):
    for axis, bit in steps:
        count = lax.axis_size(axis)
        total = total + lax.ppermute(total, axis, [(i, i ^ bit) for i in range(count)])
    return total


def bits_of(axis_sizes):
    steps = []
    for axis, count in axis_sizes:
        bit = 1
        while bit < count:
            steps.append((axis, bit))
            bit *= 2
    return steps


def passed_along(block, axis, distance):
    devices = range(lax.axis_size(axis))
    route = [(i - distance, i) for i in devices if i - distance in devices]
    return lax.ppermute(block, axis, route)


def product(pattern, left_side, right_side):
    return jnp.einsum(pattern, left_side, right_side, preferred_element_type=jnp.float32)


def tile_place(position):
    tile_number = position // TILE
    return (tile_number // GW, tile_number % GW)


def window_mask(radius, query_time, query_col, query_row, key_time, key_col, key_row, key_valid):
    apart_time = jnp.abs(query_time[:, None] - key_time[None, :])
    apart_col = jnp.abs(query_col[:, None] - key_col[None, :])
    apart_row = jnp.abs(query_row[:, None] - key_row[None, :])
    inside = apart_time[None] <= radius[:, 0, None, None]
    inside = inside & (apart_row[None] <= radius[:, 1, None, None])
    inside = inside & (apart_col[None] <= radius[:, 2, None, None])
    return inside & key_valid[None, None, :]


def normalize(raw_rows, gain_full):
    as_float = raw_rows.astype(jnp.float32)
    inverse = lax.rsqrt(jnp.mean(as_float * as_float, axis=-1, keepdims=True) + EPSILON)
    return (as_float, inverse, (as_float * inverse * gain_full).astype(jnp.bfloat16))


def normalize_back(as_float, inverse, gain_full, d_normed):
    scaled = gain_full * d_normed
    inner = jnp.mean(scaled * as_float, axis=-1, keepdims=True)
    d_raw = inverse * scaled - as_float * (inverse * inverse * inverse) * inner
    return (d_raw.astype(jnp.bfloat16), jnp.sum(d_normed * as_float * inverse, axis=0))


def forward_group(query_part, key_part, value_part, allowed, scaling):
    scores = product("qhd,khd->hqk", query_part, key_part) * scaling
    scores = jnp.where(allowed, scores, NEG_FILL)
    row_max = jnp.max(scores, axis=2, keepdims=True)
    row_sum = jnp.sum(jnp.exp(scores - row_max), axis=2, keepdims=True)
    log_sum = row_max + jnp.log(row_sum)
    weights = jnp.exp(scores - log_sum)
    weights_low = weights.astype(jnp.bfloat16)
    mixed = product("hqk,khd->qhd", weights_low, value_part)
    return (weights, weights_low, mixed, log_sum[:, :, 0])


def score_grads(weights, output_part, value_part, delta, scaling):
    d_weights = product("qhd,khd->hqk", output_part, value_part)
    return (weights * (d_weights - delta[:, :, None]) * scaling).astype(jnp.bfloat16)


def attend_chunk(query_heads, output_heads, key_ext, value_ext, windows, masks, scaling, group_size):
    own_time, own_col, own_row, ext_time, ext_col, ext_row, ext_valid = masks
    heads = query_heads.shape[1]
    mixed_parts, dq_parts, dk_parts, dv_parts = ([], [], [], [])
    for first_head in range(0, heads, group_size):
        head_range = slice(first_head, first_head + group_size)
        allowed = window_mask(
            windows[head_range], own_time, own_col, own_row, ext_time, ext_col, ext_row, ext_valid
        )
        weights, weights_low, mixed, log_sum = forward_group(
            query_heads[:, head_range],
            key_ext[:, head_range],
            value_ext[:, head_range],
            allowed,
            scaling,
        )
        delta = jnp.sum(output_heads[:, head_range] * mixed, axis=2).T
        d_scores = score_grads(
            weights, output_heads[:, head_range], value_ext[:, head_range], delta, scaling
        )
        dq_parts.append(product("hqk,khd->qhd", d_scores, key_ext[:, head_range]))
        dk_parts.append(product("hqk,qhd->khd", d_scores, query_heads[:, head_range]))
        dv_parts.append(product("hqk,qhd->khd", weights_low, output_heads[:, head_range]))
        mixed_parts.append(mixed)
    rows = query_heads.shape[0]
    width = heads * HEAD
    return (
        jnp.concatenate(mixed_parts, axis=1).reshape(rows, width),
        jnp.concatenate(dq_parts, axis=1).reshape(rows, width),
        jnp.concatenate(dk_parts, axis=1).reshape(-1, width),
        jnp.concatenate(dv_parts, axis=1).reshape(-1, width),
    )


def shards(queries, key_vectors, value_vectors, windows, gain_query, gain_key, grad_output):
    tok_rows = queries.shape[1]
    width = HEADS * HEAD
    bounds = (0, 8, HEADS) if HEADS == 20 else (0, HEADS)
    chunks = len(bounds) - 1
    group_size = 4
    key_raw = key_vectors[0]
    value_local = value_vectors[0]
    extended = [
        padded(
            jnp.stack([key_raw[:, bounds[c] * HEAD : bounds[c + 1] * HEAD],
                       value_local[:, bounds[c] * HEAD : bounds[c + 1] * HEAD]]),
            (("sp", 1),),
            tok_rows,
        )
        for c in range(chunks)
    ]
    k_float = key_raw.astype(jnp.float32)
    k_inverse = lax.rsqrt(jnp.mean(k_float * k_float, axis=-1, keepdims=True) + EPSILON)
    gains = butterfly_gather(jnp.stack([gain_query, gain_key]), "fsdp")
    k_inverse, gains = lax.optimization_barrier((k_inverse, gains))
    inverse_ext = padded(k_inverse, (("sp", 0),), tok_rows)
    lo_inverse, hi_inverse = inverse_ext[:tok_rows], inverse_ext[2 * tok_rows :]
    gain_q_full, gain_k_full = gains[0], gains[1]
    my_index = lax.axis_index("sp")
    sp_count = lax.axis_size("sp")
    scaling = HEAD ** (-0.5)
    q_float, q_inverse, q_normed = normalize(queries[0], gain_q_full)
    k_normed = (k_float * k_inverse * gain_k_full).astype(jnp.bfloat16)
    output_local = grad_output[0]
    query_heads = q_normed.reshape(tok_rows, HEADS, HEAD)
    output_heads = output_local.reshape(tok_rows, HEADS, HEAD)
    own_pos = jnp.arange(tok_rows, dtype=jnp.int32)
    own_time, own_col = tile_place(own_pos)
    own_row = jnp.zeros((tok_rows,), jnp.int32) + my_index
    ext_pos = jnp.arange(3 * tok_rows, dtype=jnp.int32)
    ext_time, ext_col = tile_place(ext_pos % tok_rows)
    ext_row = my_index - 1 + ext_pos // tok_rows
    ext_valid = (ext_row >= 0) & (ext_row < sp_count)
    masks = (own_time, own_col, own_row, ext_time, ext_col, ext_row, ext_valid)
    middle = slice(tok_rows, 2 * tok_rows)
    results, received, near_dg = [], [], []
    for c in range(chunks):
        if c > 0:
            extended[c], held = lax.optimization_barrier((extended[c], sent))
        cols = slice(bounds[c] * HEAD, bounds[c + 1] * HEAD)
        heads = slice(bounds[c], bounds[c + 1])
        chunk_heads = bounds[c + 1] - bounds[c]
        lo_float = extended[c][0, :tok_rows].astype(jnp.float32)
        hi_float = extended[c][0, 2 * tok_rows :].astype(jnp.float32)
        gain_c = gain_k_full[cols]
        key_ext = jnp.concatenate([
            (lo_float * lo_inverse * gain_c).astype(jnp.bfloat16),
            k_normed[:, cols],
            (hi_float * hi_inverse * gain_c).astype(jnp.bfloat16),
        ]).reshape(3 * tok_rows, chunk_heads, HEAD)
        value_ext = extended[c][1].reshape(3 * tok_rows, chunk_heads, HEAD)
        mixed_c, dq_c, dk_c, dv_c = attend_chunk(
            query_heads[:, heads], output_heads[:, heads], key_ext, value_ext,
            windows[heads], masks, scaling, group_size,
        )
        lower_send = jnp.stack([dk_c[:tok_rows], dv_c[:tok_rows]]).astype(jnp.bfloat16)
        upper_send = jnp.stack([dk_c[2 * tok_rows :], dv_c[2 * tok_rows :]]).astype(jnp.bfloat16)
        received.append((passed_along(lower_send, "sp", -1), passed_along(upper_send, "sp", 1)))
        sent = (lower_send, upper_send)
        results.append((mixed_c, dq_c, dk_c[middle], dv_c[middle]))
        near_dg.append(
            jnp.sum(lower_send[0].astype(jnp.float32) * lo_float * lo_inverse, axis=0)
            + jnp.sum(upper_send[0].astype(jnp.float32) * hi_float * hi_inverse, axis=0)
        )
    mixed_all = jnp.concatenate([r[0] for r in results], axis=1)
    dq_normed = jnp.concatenate([r[1] for r in results], axis=1)
    dk_own = jnp.concatenate([r[2] for r in results], axis=1)
    dv_own = jnp.concatenate([r[3] for r in results], axis=1)
    dq_out, dg_query = normalize_back(q_float, q_inverse, gain_q_full, dq_normed)
    dg_key = jnp.sum(dk_own * k_float * k_inverse, axis=0) + jnp.concatenate(near_dg)
    all_tokens = tok_rows * sp_count * lax.axis_size("clip") * lax.axis_size("fsdp")
    factor = all_tokens ** (-0.5)
    sizes = {axis: lax.axis_size(axis) for axis in ("fsdp", "clip", "sp")}
    partial_sums = jnp.stack([dg_query, dg_key])
    if all(count & (count - 1) == 0 for count in sizes.values()):
        steps = bits_of([("fsdp", sizes["fsdp"])])
        steps += [("sp", bit) for _, bit in bits_of([("sp", sizes["sp"])]) if bit > 1]
        totals = butterfly_sum(partial_sums, steps)
        received, totals = lax.optimization_barrier((received, totals))
        totals = butterfly_sum(
            totals, bits_of([("clip", sizes["clip"])]) + [("sp", 1)] * (sizes["sp"] > 1)
        )
    else:
        totals = lax.psum(partial_sums, ("fsdp", "clip", "sp"))
        received, totals = lax.optimization_barrier((received, totals))
    lower = jnp.concatenate([r[0] for r in received], axis=2).astype(jnp.float32)
    upper = jnp.concatenate([r[1] for r in received], axis=2).astype(jnp.float32)
    dk_normed = dk_own + lower[0] + upper[0]
    dv_total = dv_own + lower[1] + upper[1]
    dk_out, _ = normalize_back(k_float, k_inverse, gain_k_full, dk_normed)
    share = gain_query.shape[0]
    totals = lax.dynamic_slice_in_dim(totals, lax.axis_index("fsdp") * share, share, axis=1)
    return (
        mixed_all.astype(jnp.bfloat16)[None],
        dq_out[None],
        dk_out[None],
        dv_total.astype(jnp.bfloat16)[None],
        totals[0] * factor,
        totals[1] * factor,
    )


def solution(mesh):
    return jax.shard_map(
        shards,
        mesh=mesh,
        in_specs=(
            P(("clip", "fsdp"), "sp", None),
            P(("clip", "fsdp"), "sp", None),
            P(("clip", "fsdp"), "sp", None),
            P(),
            P("fsdp"),
            P("fsdp"),
            P(("clip", "fsdp"), "sp", None),
        ),
        out_specs=(
            P(("clip", "fsdp"), "sp", None),
            P(("clip", "fsdp"), "sp", None),
            P(("clip", "fsdp"), "sp", None),
            P(("clip", "fsdp"), "sp", None),
            P("fsdp"),
            P("fsdp"),
        ),
        check_vma=False,
    )
```

```python
import jax
import jax.numpy as jnp
from jax import lax
from jax.sharding import PartitionSpec as P

HEADS = 20
HEAD = 128
TILE = 64
GW = 1


EPSILON = 1e-06
NEG_FILL = -1e30


def padded(block, sides, width):
    for axis, dim in sides:
        count = lax.axis_size(axis)
        forward = [(i, i + 1) for i in range(count - 1)]
        backward = [(target, source) for source, target in forward]
        low = lax.ppermute(
            lax.slice_in_dim(block, block.shape[dim] - width, None, axis=dim), axis, forward
        )
        high = lax.ppermute(lax.slice_in_dim(block, 0, width, axis=dim), axis, backward)
        block = jnp.concatenate([low, block, high], axis=dim)
    return block


def butterfly_gather(block, axis):
    count = lax.axis_size(axis)
    if count & (count - 1):
        return lax.all_gather(block, axis, axis=block.ndim - 1, tiled=True)
    me = lax.axis_index(axis)
    step = 1
    while step < count:
        other = lax.ppermute(block, axis, [(i, i ^ step) for i in range(count)])
        low_first = (me // step) % 2 == 0
        block = jnp.where(
            low_first,
            jnp.concatenate([block, other], axis=-1),
            jnp.concatenate([other, block], axis=-1),
        )
        step *= 2
    return block


def butterfly_sum(total, steps):
    for axis, bit in steps:
        count = lax.axis_size(axis)
        total = total + lax.ppermute(total, axis, [(i, i ^ bit) for i in range(count)])
    return total


def bits_of(axis_sizes):
    steps = []
    for axis, count in axis_sizes:
        bit = 1
        while bit < count:
            steps.append((axis, bit))
            bit *= 2
    return steps


def four_way_sum(total, axes, high, low):
    count = 1
    for axis in axes:
        count *= lax.axis_size(axis)
    me = 0
    for axis in axes:
        me = me * lax.axis_size(axis) + lax.axis_index(axis)
    held = [total] + [
        lax.ppermute(total, axes, [(i, i ^ flip) for i in range(count)])
        for flip in (low, high, high ^ low)
    ]
    stacked = jnp.stack(held)
    place = jnp.where((me & high) != 0, 2, 0) + jnp.where((me & low) != 0, 1, 0)
    ordered = [stacked[place ^ q] for q in range(4)]
    return (ordered[0] + ordered[1]) + (ordered[2] + ordered[3])


def passed_along(block, axis, distance):
    devices = range(lax.axis_size(axis))
    route = [(i - distance, i) for i in devices if i - distance in devices]
    return lax.ppermute(block, axis, route)


def product(pattern, left_side, right_side):
    return jnp.einsum(pattern, left_side, right_side, preferred_element_type=jnp.float32)


def tile_place(position):
    tile_number = position // TILE
    return (tile_number // GW, tile_number % GW)


def window_mask(radius, query_time, query_col, query_row, key_time, key_col, key_row, key_valid):
    apart_time = jnp.abs(query_time[:, None] - key_time[None, :])
    apart_col = jnp.abs(query_col[:, None] - key_col[None, :])
    apart_row = jnp.abs(query_row[:, None] - key_row[None, :])
    inside = apart_time[None] <= radius[:, 0, None, None]
    inside = inside & (apart_row[None] <= radius[:, 1, None, None])
    inside = inside & (apart_col[None] <= radius[:, 2, None, None])
    return inside & key_valid[None, None, :]


def normalize(raw_rows, gain_full):
    as_float = raw_rows.astype(jnp.float32)
    inverse = lax.rsqrt(jnp.mean(as_float * as_float, axis=-1, keepdims=True) + EPSILON)
    return (as_float, inverse, (as_float * inverse * gain_full).astype(jnp.bfloat16))


def normalize_back(as_float, inverse, gain_full, d_normed):
    scaled = gain_full * d_normed
    inner = jnp.mean(scaled * as_float, axis=-1, keepdims=True)
    d_raw = inverse * scaled - as_float * (inverse * inverse * inverse) * inner
    return (d_raw.astype(jnp.bfloat16), jnp.sum(d_normed * as_float * inverse, axis=0))


def forward_group(query_part, key_part, value_part, allowed, scaling):
    scores = product("qhd,khd->hqk", query_part, key_part) * scaling
    scores = jnp.where(allowed, scores, NEG_FILL)
    row_max = jnp.max(scores, axis=2, keepdims=True)
    row_sum = jnp.sum(jnp.exp(scores - row_max), axis=2, keepdims=True)
    log_sum = row_max + jnp.log(row_sum)
    weights = jnp.exp(scores - log_sum)
    weights_low = weights.astype(jnp.bfloat16)
    mixed = product("hqk,khd->qhd", weights_low, value_part)
    return (weights, weights_low, mixed, log_sum[:, :, 0])


def score_grads(weights, output_part, value_part, delta, scaling):
    d_weights = product("qhd,khd->hqk", output_part, value_part)
    return (weights * (d_weights - delta[:, :, None]) * scaling).astype(jnp.bfloat16)


def attend_chunk(query_heads, output_heads, key_ext, value_ext, windows, masks, scaling, group_size):
    own_time, own_col, own_row, ext_time, ext_col, ext_row, ext_valid = masks
    heads = query_heads.shape[1]
    mixed_parts, dq_parts, dk_parts, dv_parts = ([], [], [], [])
    for first_head in range(0, heads, group_size):
        head_range = slice(first_head, first_head + group_size)
        allowed = window_mask(
            windows[head_range], own_time, own_col, own_row, ext_time, ext_col, ext_row, ext_valid
        )
        weights, weights_low, mixed, log_sum = forward_group(
            query_heads[:, head_range],
            key_ext[:, head_range],
            value_ext[:, head_range],
            allowed,
            scaling,
        )
        delta = jnp.sum(output_heads[:, head_range] * mixed, axis=2).T
        d_scores = score_grads(
            weights, output_heads[:, head_range], value_ext[:, head_range], delta, scaling
        )
        dq_parts.append(product("hqk,khd->qhd", d_scores, key_ext[:, head_range]))
        dk_parts.append(product("hqk,qhd->khd", d_scores, query_heads[:, head_range]))
        dv_parts.append(product("hqk,qhd->khd", weights_low, output_heads[:, head_range]))
        mixed_parts.append(mixed)
    rows = query_heads.shape[0]
    width = heads * HEAD
    return (
        jnp.concatenate(mixed_parts, axis=1).reshape(rows, width),
        jnp.concatenate(dq_parts, axis=1).reshape(rows, width),
        jnp.concatenate(dk_parts, axis=1).reshape(-1, width),
        jnp.concatenate(dv_parts, axis=1).reshape(-1, width),
    )


def shards(queries, key_vectors, value_vectors, windows, gain_query, gain_key, grad_output):
    tok_rows = queries.shape[1]
    width = HEADS * HEAD
    bounds = (0, 8, HEADS) if HEADS == 20 else (0, HEADS)
    chunks = len(bounds) - 1
    group_size = 4
    key_raw = key_vectors[0]
    value_local = value_vectors[0]
    extended = [
        padded(
            jnp.stack([key_raw[:, bounds[c] * HEAD : bounds[c + 1] * HEAD],
                       value_local[:, bounds[c] * HEAD : bounds[c + 1] * HEAD]]),
            (("sp", 1),),
            tok_rows,
        )
        for c in range(chunks)
    ]
    k_float = key_raw.astype(jnp.float32)
    k_inverse = lax.rsqrt(jnp.mean(k_float * k_float, axis=-1, keepdims=True) + EPSILON)
    gains = butterfly_gather(jnp.stack([gain_query, gain_key]), "fsdp")
    k_inverse, gains = lax.optimization_barrier((k_inverse, gains))
    inverse_ext = padded(k_inverse, (("sp", 0),), tok_rows)
    lo_inverse, hi_inverse = inverse_ext[:tok_rows], inverse_ext[2 * tok_rows :]
    gain_q_full, gain_k_full = gains[0], gains[1]
    my_index = lax.axis_index("sp")
    sp_count = lax.axis_size("sp")
    scaling = HEAD ** (-0.5)
    q_float, q_inverse, q_normed = normalize(queries[0], gain_q_full)
    k_normed = (k_float * k_inverse * gain_k_full).astype(jnp.bfloat16)
    output_local = grad_output[0]
    query_heads = q_normed.reshape(tok_rows, HEADS, HEAD)
    output_heads = output_local.reshape(tok_rows, HEADS, HEAD)
    own_pos = jnp.arange(tok_rows, dtype=jnp.int32)
    own_time, own_col = tile_place(own_pos)
    own_row = jnp.zeros((tok_rows,), jnp.int32) + my_index
    ext_pos = jnp.arange(3 * tok_rows, dtype=jnp.int32)
    ext_time, ext_col = tile_place(ext_pos % tok_rows)
    ext_row = my_index - 1 + ext_pos // tok_rows
    ext_valid = (ext_row >= 0) & (ext_row < sp_count)
    masks = (own_time, own_col, own_row, ext_time, ext_col, ext_row, ext_valid)
    middle = slice(tok_rows, 2 * tok_rows)
    results, received, near_dg = [], [], []
    for c in range(chunks):
        if c > 0:
            extended[c], held = lax.optimization_barrier((extended[c], sent))
        cols = slice(bounds[c] * HEAD, bounds[c + 1] * HEAD)
        heads = slice(bounds[c], bounds[c + 1])
        chunk_heads = bounds[c + 1] - bounds[c]
        lo_float = extended[c][0, :tok_rows].astype(jnp.float32)
        hi_float = extended[c][0, 2 * tok_rows :].astype(jnp.float32)
        gain_c = gain_k_full[cols]
        key_ext = jnp.concatenate([
            (lo_float * lo_inverse * gain_c).astype(jnp.bfloat16),
            k_normed[:, cols],
            (hi_float * hi_inverse * gain_c).astype(jnp.bfloat16),
        ]).reshape(3 * tok_rows, chunk_heads, HEAD)
        value_ext = extended[c][1].reshape(3 * tok_rows, chunk_heads, HEAD)
        mixed_c, dq_c, dk_c, dv_c = attend_chunk(
            query_heads[:, heads], output_heads[:, heads], key_ext, value_ext,
            windows[heads], masks, scaling, group_size,
        )
        lower_send = jnp.stack([dk_c[:tok_rows], dv_c[:tok_rows]]).astype(jnp.bfloat16)
        upper_send = jnp.stack([dk_c[2 * tok_rows :], dv_c[2 * tok_rows :]]).astype(jnp.bfloat16)
        received.append((passed_along(lower_send, "sp", -1), passed_along(upper_send, "sp", 1)))
        sent = (lower_send, upper_send)
        results.append((mixed_c, dq_c, dk_c[middle], dv_c[middle]))
        near_dg.append(
            jnp.sum(lower_send[0].astype(jnp.float32) * lo_float * lo_inverse, axis=0)
            + jnp.sum(upper_send[0].astype(jnp.float32) * hi_float * hi_inverse, axis=0)
        )
    mixed_all = jnp.concatenate([r[0] for r in results], axis=1)
    dq_normed = jnp.concatenate([r[1] for r in results], axis=1)
    dk_own = jnp.concatenate([r[2] for r in results], axis=1)
    dv_own = jnp.concatenate([r[3] for r in results], axis=1)
    dq_out, dg_query = normalize_back(q_float, q_inverse, gain_q_full, dq_normed)
    dg_key = jnp.sum(dk_own * k_float * k_inverse, axis=0) + jnp.concatenate(near_dg)
    all_tokens = tok_rows * sp_count * lax.axis_size("clip") * lax.axis_size("fsdp")
    factor = all_tokens ** (-0.5)
    sizes = {axis: lax.axis_size(axis) for axis in ("fsdp", "clip", "sp")}
    partial_sums = jnp.stack([dg_query, dg_key])
    if all(count & (count - 1) == 0 for count in sizes.values()):
        steps = bits_of([("fsdp", sizes["fsdp"])])
        steps += [("sp", bit) for _, bit in bits_of([("sp", sizes["sp"])]) if bit > 1]
        totals = butterfly_sum(partial_sums, steps)
        received, totals = lax.optimization_barrier((received, totals))
        if sizes["clip"] == 2 and sizes["sp"] > 1:
            totals = four_way_sum(totals, ("clip", "sp"), sizes["sp"], 1)
        else:
            totals = butterfly_sum(
                totals, bits_of([("clip", sizes["clip"])]) + [("sp", 1)] * (sizes["sp"] > 1)
            )
    else:
        totals = lax.psum(partial_sums, ("fsdp", "clip", "sp"))
        received, totals = lax.optimization_barrier((received, totals))
    lower = jnp.concatenate([r[0] for r in received], axis=2).astype(jnp.float32)
    upper = jnp.concatenate([r[1] for r in received], axis=2).astype(jnp.float32)
    dk_normed = dk_own + lower[0] + upper[0]
    dv_total = dv_own + lower[1] + upper[1]
    dk_out, _ = normalize_back(k_float, k_inverse, gain_k_full, dk_normed)
    share = gain_query.shape[0]
    totals = lax.dynamic_slice_in_dim(totals, lax.axis_index("fsdp") * share, share, axis=1)
    return (
        mixed_all.astype(jnp.bfloat16)[None],
        dq_out[None],
        dk_out[None],
        dv_total.astype(jnp.bfloat16)[None],
        totals[0] * factor,
        totals[1] * factor,
    )


def solution(mesh):
    return jax.shard_map(
        shards,
        mesh=mesh,
        in_specs=(
            P(("clip", "fsdp"), "sp", None),
            P(("clip", "fsdp"), "sp", None),
            P(("clip", "fsdp"), "sp", None),
            P(),
            P("fsdp"),
            P("fsdp"),
            P(("clip", "fsdp"), "sp", None),
        ),
        out_specs=(
            P(("clip", "fsdp"), "sp", None),
            P(("clip", "fsdp"), "sp", None),
            P(("clip", "fsdp"), "sp", None),
            P(("clip", "fsdp"), "sp", None),
            P("fsdp"),
            P("fsdp"),
        ),
        check_vma=False,
    )
```

```python
import jax
import jax.numpy as jnp
from jax import lax
from jax.sharding import PartitionSpec as P

HEADS = 20
HEAD = 128
TILE = 64
GW = 1


EPSILON = 1e-06
NEG_FILL = -1e30


def padded(block, sides, width):
    for axis, dim in sides:
        count = lax.axis_size(axis)
        forward = [(i, i + 1) for i in range(count - 1)]
        backward = [(target, source) for source, target in forward]
        low = lax.ppermute(
            lax.slice_in_dim(block, block.shape[dim] - width, None, axis=dim), axis, forward
        )
        high = lax.ppermute(lax.slice_in_dim(block, 0, width, axis=dim), axis, backward)
        block = jnp.concatenate([low, block, high], axis=dim)
    return block


def butterfly_gather(block, axis):
    count = lax.axis_size(axis)
    if count & (count - 1):
        return lax.all_gather(block, axis, axis=block.ndim - 1, tiled=True)
    me = lax.axis_index(axis)
    step = 1
    while step < count:
        other = lax.ppermute(block, axis, [(i, i ^ step) for i in range(count)])
        low_first = (me // step) % 2 == 0
        block = jnp.where(
            low_first,
            jnp.concatenate([block, other], axis=-1),
            jnp.concatenate([other, block], axis=-1),
        )
        step *= 2
    return block


def butterfly_sum(total, steps):
    for axis, bit in steps:
        count = lax.axis_size(axis)
        total = total + lax.ppermute(total, axis, [(i, i ^ bit) for i in range(count)])
    return total


def bits_of(axis_sizes):
    steps = []
    for axis, count in axis_sizes:
        bit = 1
        while bit < count:
            steps.append((axis, bit))
            bit *= 2
    return steps


def passed_along(block, axis, distance):
    devices = range(lax.axis_size(axis))
    route = [(i - distance, i) for i in devices if i - distance in devices]
    return lax.ppermute(block, axis, route)


def product(pattern, left_side, right_side):
    return jnp.einsum(pattern, left_side, right_side, preferred_element_type=jnp.float32)


def tile_place(position):
    tile_number = position // TILE
    return (tile_number // GW, tile_number % GW)


def window_mask(radius, query_time, query_col, query_row, key_time, key_col, key_row, key_valid):
    apart_time = jnp.abs(query_time[:, None] - key_time[None, :])
    apart_col = jnp.abs(query_col[:, None] - key_col[None, :])
    apart_row = jnp.abs(query_row[:, None] - key_row[None, :])
    inside = apart_time[None] <= radius[:, 0, None, None]
    inside = inside & (apart_row[None] <= radius[:, 1, None, None])
    inside = inside & (apart_col[None] <= radius[:, 2, None, None])
    return inside & key_valid[None, None, :]


def normalize(raw_rows, gain_full):
    as_float = raw_rows.astype(jnp.float32)
    inverse = lax.rsqrt(jnp.mean(as_float * as_float, axis=-1, keepdims=True) + EPSILON)
    return (as_float, inverse, (as_float * inverse * gain_full).astype(jnp.bfloat16))


def normalize_back(as_float, inverse, gain_full, d_normed):
    scaled = gain_full * d_normed
    inner = jnp.mean(scaled * as_float, axis=-1, keepdims=True)
    d_raw = inverse * scaled - as_float * (inverse * inverse * inverse) * inner
    return (d_raw.astype(jnp.bfloat16), jnp.sum(d_normed * as_float * inverse, axis=0))


def forward_group(query_part, key_part, value_part, allowed, scaling):
    scores = product("qhd,khd->hqk", query_part, key_part) * scaling
    scores = jnp.where(allowed, scores, NEG_FILL)
    row_max = jnp.max(scores, axis=2, keepdims=True)
    row_sum = jnp.sum(jnp.exp(scores - row_max), axis=2, keepdims=True)
    log_sum = row_max + jnp.log(row_sum)
    weights = jnp.exp(scores - log_sum)
    weights_low = weights.astype(jnp.bfloat16)
    mixed = product("hqk,khd->qhd", weights_low, value_part)
    return (weights, weights_low, mixed, log_sum[:, :, 0])


def score_grads(weights, output_part, value_part, delta, scaling):
    d_weights = product("qhd,khd->hqk", output_part, value_part)
    return (weights * (d_weights - delta[:, :, None]) * scaling).astype(jnp.bfloat16)


def attend_chunk(query_heads, output_heads, key_ext, value_ext, windows, masks, scaling, group_size):
    own_time, own_col, own_row, ext_time, ext_col, ext_row, ext_valid = masks
    heads = query_heads.shape[1]
    mixed_parts, dq_parts, dk_parts, dv_parts = ([], [], [], [])
    for first_head in range(0, heads, group_size):
        head_range = slice(first_head, first_head + group_size)
        allowed = window_mask(
            windows[head_range], own_time, own_col, own_row, ext_time, ext_col, ext_row, ext_valid
        )
        weights, weights_low, mixed, log_sum = forward_group(
            query_heads[:, head_range],
            key_ext[:, head_range],
            value_ext[:, head_range],
            allowed,
            scaling,
        )
        delta = jnp.sum(output_heads[:, head_range] * mixed, axis=2).T
        d_scores = score_grads(
            weights, output_heads[:, head_range], value_ext[:, head_range], delta, scaling
        )
        dq_parts.append(product("hqk,khd->qhd", d_scores, key_ext[:, head_range]))
        dk_parts.append(product("hqk,qhd->khd", d_scores, query_heads[:, head_range]))
        dv_parts.append(product("hqk,qhd->khd", weights_low, output_heads[:, head_range]))
        mixed_parts.append(mixed)
    rows = query_heads.shape[0]
    width = heads * HEAD
    return (
        jnp.concatenate(mixed_parts, axis=1).reshape(rows, width),
        jnp.concatenate(dq_parts, axis=1).reshape(rows, width),
        jnp.concatenate(dk_parts, axis=1).reshape(-1, width),
        jnp.concatenate(dv_parts, axis=1).reshape(-1, width),
    )


def shards(queries, key_vectors, value_vectors, windows, gain_query, gain_key, grad_output):
    tok_rows = queries.shape[1]
    width = HEADS * HEAD
    bounds = (0, 8, HEADS) if HEADS == 20 else (0, HEADS)
    chunks = len(bounds) - 1
    key_raw = key_vectors[0]
    value_local = value_vectors[0]
    extended = [
        padded(
            jnp.stack([key_raw[:, bounds[c] * HEAD : bounds[c + 1] * HEAD],
                       value_local[:, bounds[c] * HEAD : bounds[c + 1] * HEAD]]),
            (("sp", 1),),
            tok_rows,
        )
        for c in range(chunks)
    ]
    k_float = key_raw.astype(jnp.float32)
    k_inverse = lax.rsqrt(jnp.mean(k_float * k_float, axis=-1, keepdims=True) + EPSILON)
    gains = butterfly_gather(jnp.stack([gain_query, gain_key]), "fsdp")
    k_inverse, gains = lax.optimization_barrier((k_inverse, gains))
    inverse_ext = padded(k_inverse, (("sp", 0),), tok_rows)
    lo_inverse, hi_inverse = inverse_ext[:tok_rows], inverse_ext[2 * tok_rows :]
    gain_q_full, gain_k_full = gains[0], gains[1]
    my_index = lax.axis_index("sp")
    sp_count = lax.axis_size("sp")
    scaling = HEAD ** (-0.5)
    q_float, q_inverse, q_normed = normalize(queries[0], gain_q_full)
    k_normed = (k_float * k_inverse * gain_k_full).astype(jnp.bfloat16)
    output_local = grad_output[0]
    query_heads = q_normed.reshape(tok_rows, HEADS, HEAD)
    output_heads = output_local.reshape(tok_rows, HEADS, HEAD)
    own_pos = jnp.arange(tok_rows, dtype=jnp.int32)
    own_time, own_col = tile_place(own_pos)
    own_row = jnp.zeros((tok_rows,), jnp.int32) + my_index
    ext_pos = jnp.arange(3 * tok_rows, dtype=jnp.int32)
    ext_time, ext_col = tile_place(ext_pos % tok_rows)
    ext_row = my_index - 1 + ext_pos // tok_rows
    ext_valid = (ext_row >= 0) & (ext_row < sp_count)
    masks = (own_time, own_col, own_row, ext_time, ext_col, ext_row, ext_valid)
    middle = slice(tok_rows, 2 * tok_rows)
    results, received, near_dg = [], [], []
    for c in range(chunks):
        if c > 0:
            extended[c], held = lax.optimization_barrier((extended[c], sent))
        cols = slice(bounds[c] * HEAD, bounds[c + 1] * HEAD)
        heads = slice(bounds[c], bounds[c + 1])
        chunk_heads = bounds[c + 1] - bounds[c]
        lo_float = extended[c][0, :tok_rows].astype(jnp.float32)
        hi_float = extended[c][0, 2 * tok_rows :].astype(jnp.float32)
        gain_c = gain_k_full[cols]
        key_ext = jnp.concatenate([
            (lo_float * lo_inverse * gain_c).astype(jnp.bfloat16),
            k_normed[:, cols],
            (hi_float * hi_inverse * gain_c).astype(jnp.bfloat16),
        ]).reshape(3 * tok_rows, chunk_heads, HEAD)
        value_ext = extended[c][1].reshape(3 * tok_rows, chunk_heads, HEAD)
        mixed_c, dq_c, dk_c, dv_c = attend_chunk(
            query_heads[:, heads], output_heads[:, heads], key_ext, value_ext,
            windows[heads], masks, scaling, chunk_heads,
        )
        lower_send = jnp.stack([dk_c[:tok_rows], dv_c[:tok_rows]]).astype(jnp.bfloat16)
        upper_send = jnp.stack([dk_c[2 * tok_rows :], dv_c[2 * tok_rows :]]).astype(jnp.bfloat16)
        received.append((passed_along(lower_send, "sp", -1), passed_along(upper_send, "sp", 1)))
        sent = (lower_send, upper_send)
        results.append((mixed_c, dq_c, dk_c[middle], dv_c[middle]))
        near_dg.append(
            jnp.sum(lower_send[0].astype(jnp.float32) * lo_float * lo_inverse, axis=0)
            + jnp.sum(upper_send[0].astype(jnp.float32) * hi_float * hi_inverse, axis=0)
        )
    mixed_all = jnp.concatenate([r[0] for r in results], axis=1)
    dq_normed = jnp.concatenate([r[1] for r in results], axis=1)
    dk_own = jnp.concatenate([r[2] for r in results], axis=1)
    dv_own = jnp.concatenate([r[3] for r in results], axis=1)
    dq_out, dg_query = normalize_back(q_float, q_inverse, gain_q_full, dq_normed)
    dg_key = jnp.sum(dk_own * k_float * k_inverse, axis=0) + jnp.concatenate(near_dg)
    all_tokens = tok_rows * sp_count * lax.axis_size("clip") * lax.axis_size("fsdp")
    factor = all_tokens ** (-0.5)
    sizes = {axis: lax.axis_size(axis) for axis in ("fsdp", "clip", "sp")}
    partial_sums = jnp.stack([dg_query, dg_key])
    if all(count & (count - 1) == 0 for count in sizes.values()):
        steps = bits_of([("fsdp", sizes["fsdp"])])
        steps += [("sp", bit) for _, bit in bits_of([("sp", sizes["sp"])]) if bit > 1]
        totals = butterfly_sum(partial_sums, steps)
        received, totals = lax.optimization_barrier((received, totals))
        totals = butterfly_sum(
            totals, bits_of([("clip", sizes["clip"])]) + [("sp", 1)] * (sizes["sp"] > 1)
        )
    else:
        totals = lax.psum(partial_sums, ("fsdp", "clip", "sp"))
        received, totals = lax.optimization_barrier((received, totals))
    lower = jnp.concatenate([r[0] for r in received], axis=2).astype(jnp.float32)
    upper = jnp.concatenate([r[1] for r in received], axis=2).astype(jnp.float32)
    dk_normed = dk_own + lower[0] + upper[0]
    dv_total = dv_own + lower[1] + upper[1]
    dk_out, _ = normalize_back(k_float, k_inverse, gain_k_full, dk_normed)
    share = gain_query.shape[0]
    totals = lax.dynamic_slice_in_dim(totals, lax.axis_index("fsdp") * share, share, axis=1)
    return (
        mixed_all.astype(jnp.bfloat16)[None],
        dq_out[None],
        dk_out[None],
        dv_total.astype(jnp.bfloat16)[None],
        totals[0] * factor,
        totals[1] * factor,
    )


def solution(mesh):
    return jax.shard_map(
        shards,
        mesh=mesh,
        in_specs=(
            P(("clip", "fsdp"), "sp", None),
            P(("clip", "fsdp"), "sp", None),
            P(("clip", "fsdp"), "sp", None),
            P(),
            P("fsdp"),
            P("fsdp"),
            P(("clip", "fsdp"), "sp", None),
        ),
        out_specs=(
            P(("clip", "fsdp"), "sp", None),
            P(("clip", "fsdp"), "sp", None),
            P(("clip", "fsdp"), "sp", None),
            P(("clip", "fsdp"), "sp", None),
            P("fsdp"),
            P("fsdp"),
        ),
        check_vma=False,
    )
```

```python
import jax
import jax.numpy as jnp
from jax import lax
from jax.sharding import PartitionSpec as P

HEADS = 20
HEAD = 128
TILE = 64
GW = 1


EPSILON = 1e-06
NEG_FILL = -1e30


def padded(block, sides, width):
    for axis, dim in sides:
        count = lax.axis_size(axis)
        forward = [(i, i + 1) for i in range(count - 1)]
        backward = [(target, source) for source, target in forward]
        low = lax.ppermute(
            lax.slice_in_dim(block, block.shape[dim] - width, None, axis=dim), axis, forward
        )
        high = lax.ppermute(lax.slice_in_dim(block, 0, width, axis=dim), axis, backward)
        block = jnp.concatenate([low, block, high], axis=dim)
    return block


def butterfly_gather(block, axis):
    count = lax.axis_size(axis)
    if count & (count - 1):
        return lax.all_gather(block, axis, axis=block.ndim - 1, tiled=True)
    me = lax.axis_index(axis)
    step = 1
    while step < count:
        other = lax.ppermute(block, axis, [(i, i ^ step) for i in range(count)])
        low_first = (me // step) % 2 == 0
        block = jnp.where(
            low_first,
            jnp.concatenate([block, other], axis=-1),
            jnp.concatenate([other, block], axis=-1),
        )
        step *= 2
    return block


def butterfly_sum(total, steps):
    for axis, bit in steps:
        count = lax.axis_size(axis)
        total = total + lax.ppermute(total, axis, [(i, i ^ bit) for i in range(count)])
    return total


def bits_of(axis_sizes):
    steps = []
    for axis, count in axis_sizes:
        bit = 1
        while bit < count:
            steps.append((axis, bit))
            bit *= 2
    return steps


def passed_along(block, axis, distance):
    devices = range(lax.axis_size(axis))
    route = [(i - distance, i) for i in devices if i - distance in devices]
    return lax.ppermute(block, axis, route)


def product(pattern, left_side, right_side):
    return jnp.einsum(pattern, left_side, right_side, preferred_element_type=jnp.float32)


def tile_place(position):
    tile_number = position // TILE
    return (tile_number // GW, tile_number % GW)


def window_mask(radius, query_time, query_col, query_row, key_time, key_col, key_row, key_valid):
    apart_time = jnp.abs(query_time[:, None] - key_time[None, :])
    apart_col = jnp.abs(query_col[:, None] - key_col[None, :])
    apart_row = jnp.abs(query_row[:, None] - key_row[None, :])
    inside = apart_time[None] <= radius[:, 0, None, None]
    inside = inside & (apart_row[None] <= radius[:, 1, None, None])
    inside = inside & (apart_col[None] <= radius[:, 2, None, None])
    return inside & key_valid[None, None, :]


def normalize(raw_rows, gain_full):
    as_float = raw_rows.astype(jnp.float32)
    inverse = lax.rsqrt(jnp.mean(as_float * as_float, axis=-1, keepdims=True) + EPSILON)
    return (as_float, inverse, (as_float * inverse * gain_full).astype(jnp.bfloat16))


def normalize_back(as_float, inverse, gain_full, d_normed):
    scaled = gain_full * d_normed
    inner = jnp.mean(scaled * as_float, axis=-1, keepdims=True)
    d_raw = inverse * scaled - as_float * (inverse * inverse * inverse) * inner
    return (d_raw.astype(jnp.bfloat16), jnp.sum(d_normed * as_float * inverse, axis=0))


def forward_group(query_part, key_part, value_part, allowed, scaling):
    scores = product("qhd,khd->hqk", query_part, key_part) * scaling
    scores = jnp.where(allowed, scores, NEG_FILL)
    row_max = jnp.max(scores, axis=2, keepdims=True)
    row_sum = jnp.sum(jnp.exp(scores - row_max), axis=2, keepdims=True)
    log_sum = row_max + jnp.log(row_sum)
    weights = jnp.exp(scores - log_sum)
    weights_low = weights.astype(jnp.bfloat16)
    mixed = product("hqk,khd->qhd", weights_low, value_part)
    return (weights, weights_low, mixed, log_sum[:, :, 0])


def score_grads(weights, output_part, value_part, delta, scaling):
    d_weights = product("qhd,khd->hqk", output_part, value_part)
    return (weights * (d_weights - delta[:, :, None]) * scaling).astype(jnp.bfloat16)


def attend_chunk(query_heads, output_heads, key_ext, value_ext, windows, masks, scaling, group_size):
    own_time, own_col, own_row, ext_time, ext_col, ext_row, ext_valid = masks
    heads = query_heads.shape[1]
    mixed_parts, dq_parts, dk_parts, dv_parts = ([], [], [], [])
    for first_head in range(0, heads, group_size):
        head_range = slice(first_head, first_head + group_size)
        allowed = window_mask(
            windows[head_range], own_time, own_col, own_row, ext_time, ext_col, ext_row, ext_valid
        )
        weights, weights_low, mixed, log_sum = forward_group(
            query_heads[:, head_range],
            key_ext[:, head_range],
            value_ext[:, head_range],
            allowed,
            scaling,
        )
        delta = jnp.sum(output_heads[:, head_range] * mixed, axis=2).T
        d_scores = score_grads(
            weights, output_heads[:, head_range], value_ext[:, head_range], delta, scaling
        )
        dq_parts.append(product("hqk,khd->qhd", d_scores, key_ext[:, head_range]))
        dk_parts.append(product("hqk,qhd->khd", d_scores, query_heads[:, head_range]))
        dv_parts.append(product("hqk,qhd->khd", weights_low, output_heads[:, head_range]))
        mixed_parts.append(mixed)
    rows = query_heads.shape[0]
    width = heads * HEAD
    return (
        jnp.concatenate(mixed_parts, axis=1).reshape(rows, width),
        jnp.concatenate(dq_parts, axis=1).reshape(rows, width),
        jnp.concatenate(dk_parts, axis=1).reshape(-1, width),
        jnp.concatenate(dv_parts, axis=1).reshape(-1, width),
    )


def shards(queries, key_vectors, value_vectors, windows, gain_query, gain_key, grad_output):
    tok_rows = queries.shape[1]
    width = HEADS * HEAD
    bounds = (0, 9, HEADS) if HEADS == 20 else (0, HEADS)
    chunks = len(bounds) - 1
    key_raw = key_vectors[0]
    value_local = value_vectors[0]
    extended = [
        padded(
            jnp.stack([key_raw[:, bounds[c] * HEAD : bounds[c + 1] * HEAD],
                       value_local[:, bounds[c] * HEAD : bounds[c + 1] * HEAD]]),
            (("sp", 1),),
            tok_rows,
        )
        for c in range(chunks)
    ]
    k_float = key_raw.astype(jnp.float32)
    k_inverse = lax.rsqrt(jnp.mean(k_float * k_float, axis=-1, keepdims=True) + EPSILON)
    gains = butterfly_gather(jnp.stack([gain_query, gain_key]), "fsdp")
    k_inverse, gains = lax.optimization_barrier((k_inverse, gains))
    inverse_ext = padded(k_inverse, (("sp", 0),), tok_rows)
    lo_inverse, hi_inverse = inverse_ext[:tok_rows], inverse_ext[2 * tok_rows :]
    gain_q_full, gain_k_full = gains[0], gains[1]
    my_index = lax.axis_index("sp")
    sp_count = lax.axis_size("sp")
    scaling = HEAD ** (-0.5)
    q_float, q_inverse, q_normed = normalize(queries[0], gain_q_full)
    k_normed = (k_float * k_inverse * gain_k_full).astype(jnp.bfloat16)
    output_local = grad_output[0]
    query_heads = q_normed.reshape(tok_rows, HEADS, HEAD)
    output_heads = output_local.reshape(tok_rows, HEADS, HEAD)
    own_pos = jnp.arange(tok_rows, dtype=jnp.int32)
    own_time, own_col = tile_place(own_pos)
    own_row = jnp.zeros((tok_rows,), jnp.int32) + my_index
    ext_pos = jnp.arange(3 * tok_rows, dtype=jnp.int32)
    ext_time, ext_col = tile_place(ext_pos % tok_rows)
    ext_row = my_index - 1 + ext_pos // tok_rows
    ext_valid = (ext_row >= 0) & (ext_row < sp_count)
    masks = (own_time, own_col, own_row, ext_time, ext_col, ext_row, ext_valid)
    middle = slice(tok_rows, 2 * tok_rows)
    results, received, near_dg = [], [], []
    for c in range(chunks):
        if c > 0:
            extended[c], held = lax.optimization_barrier((extended[c], sent))
        cols = slice(bounds[c] * HEAD, bounds[c + 1] * HEAD)
        heads = slice(bounds[c], bounds[c + 1])
        chunk_heads = bounds[c + 1] - bounds[c]
        lo_float = extended[c][0, :tok_rows].astype(jnp.float32)
        hi_float = extended[c][0, 2 * tok_rows :].astype(jnp.float32)
        gain_c = gain_k_full[cols]
        key_ext = jnp.concatenate([
            (lo_float * lo_inverse * gain_c).astype(jnp.bfloat16),
            k_normed[:, cols],
            (hi_float * hi_inverse * gain_c).astype(jnp.bfloat16),
        ]).reshape(3 * tok_rows, chunk_heads, HEAD)
        value_ext = extended[c][1].reshape(3 * tok_rows, chunk_heads, HEAD)
        mixed_c, dq_c, dk_c, dv_c = attend_chunk(
            query_heads[:, heads], output_heads[:, heads], key_ext, value_ext,
            windows[heads], masks, scaling, chunk_heads,
        )
        lower_send = jnp.stack([dk_c[:tok_rows], dv_c[:tok_rows]]).astype(jnp.bfloat16)
        upper_send = jnp.stack([dk_c[2 * tok_rows :], dv_c[2 * tok_rows :]]).astype(jnp.bfloat16)
        received.append((passed_along(lower_send, "sp", -1), passed_along(upper_send, "sp", 1)))
        sent = (lower_send, upper_send)
        results.append((mixed_c, dq_c, dk_c[middle], dv_c[middle]))
        near_dg.append(
            jnp.sum(lower_send[0].astype(jnp.float32) * lo_float * lo_inverse, axis=0)
            + jnp.sum(upper_send[0].astype(jnp.float32) * hi_float * hi_inverse, axis=0)
        )
    mixed_all = jnp.concatenate([r[0] for r in results], axis=1)
    dq_normed = jnp.concatenate([r[1] for r in results], axis=1)
    dk_own = jnp.concatenate([r[2] for r in results], axis=1)
    dv_own = jnp.concatenate([r[3] for r in results], axis=1)
    dq_out, dg_query = normalize_back(q_float, q_inverse, gain_q_full, dq_normed)
    dg_key = jnp.sum(dk_own * k_float * k_inverse, axis=0) + jnp.concatenate(near_dg)
    all_tokens = tok_rows * sp_count * lax.axis_size("clip") * lax.axis_size("fsdp")
    factor = all_tokens ** (-0.5)
    sizes = {axis: lax.axis_size(axis) for axis in ("fsdp", "clip", "sp")}
    partial_sums = jnp.stack([dg_query, dg_key])
    if all(count & (count - 1) == 0 for count in sizes.values()):
        steps = bits_of([("fsdp", sizes["fsdp"])])
        steps += [("sp", bit) for _, bit in bits_of([("sp", sizes["sp"])]) if bit > 1]
        totals = butterfly_sum(partial_sums, steps)
        received, totals = lax.optimization_barrier((received, totals))
        totals = butterfly_sum(
            totals, bits_of([("clip", sizes["clip"])]) + [("sp", 1)] * (sizes["sp"] > 1)
        )
    else:
        totals = lax.psum(partial_sums, ("fsdp", "clip", "sp"))
        received, totals = lax.optimization_barrier((received, totals))
    lower = jnp.concatenate([r[0] for r in received], axis=2).astype(jnp.float32)
    upper = jnp.concatenate([r[1] for r in received], axis=2).astype(jnp.float32)
    dk_normed = dk_own + lower[0] + upper[0]
    dv_total = dv_own + lower[1] + upper[1]
    dk_out, _ = normalize_back(k_float, k_inverse, gain_k_full, dk_normed)
    share = gain_query.shape[0]
    totals = lax.dynamic_slice_in_dim(totals, lax.axis_index("fsdp") * share, share, axis=1)
    return (
        mixed_all.astype(jnp.bfloat16)[None],
        dq_out[None],
        dk_out[None],
        dv_total.astype(jnp.bfloat16)[None],
        totals[0] * factor,
        totals[1] * factor,
    )


def solution(mesh):
    return jax.shard_map(
        shards,
        mesh=mesh,
        in_specs=(
            P(("clip", "fsdp"), "sp", None),
            P(("clip", "fsdp"), "sp", None),
            P(("clip", "fsdp"), "sp", None),
            P(),
            P("fsdp"),
            P("fsdp"),
            P(("clip", "fsdp"), "sp", None),
        ),
        out_specs=(
            P(("clip", "fsdp"), "sp", None),
            P(("clip", "fsdp"), "sp", None),
            P(("clip", "fsdp"), "sp", None),
            P(("clip", "fsdp"), "sp", None),
            P("fsdp"),
            P("fsdp"),
        ),
        check_vma=False,
    )
```

```python
import jax
import jax.numpy as jnp
from jax import lax
from jax.sharding import PartitionSpec as P

HEADS = 20
HEAD = 128
TILE = 64
GW = 1


EPSILON = 1e-06
NEG_FILL = -1e30


def padded(block, sides, width):
    for axis, dim in sides:
        count = lax.axis_size(axis)
        forward = [(i, i + 1) for i in range(count - 1)]
        backward = [(target, source) for source, target in forward]
        low = lax.ppermute(
            lax.slice_in_dim(block, block.shape[dim] - width, None, axis=dim), axis, forward
        )
        high = lax.ppermute(lax.slice_in_dim(block, 0, width, axis=dim), axis, backward)
        block = jnp.concatenate([low, block, high], axis=dim)
    return block


def butterfly_gather(block, axis):
    count = lax.axis_size(axis)
    if count & (count - 1):
        return lax.all_gather(block, axis, axis=block.ndim - 1, tiled=True)
    me = lax.axis_index(axis)
    step = 1
    while step < count:
        other = lax.ppermute(block, axis, [(i, i ^ step) for i in range(count)])
        low_first = (me // step) % 2 == 0
        block = jnp.where(
            low_first,
            jnp.concatenate([block, other], axis=-1),
            jnp.concatenate([other, block], axis=-1),
        )
        step *= 2
    return block


def butterfly_sum(total, steps):
    for axis, bit in steps:
        count = lax.axis_size(axis)
        total = total + lax.ppermute(total, axis, [(i, i ^ bit) for i in range(count)])
    return total


def bits_of(axis_sizes):
    steps = []
    for axis, count in axis_sizes:
        bit = 1
        while bit < count:
            steps.append((axis, bit))
            bit *= 2
    return steps


def passed_along(block, axis, distance):
    devices = range(lax.axis_size(axis))
    route = [(i - distance, i) for i in devices if i - distance in devices]
    return lax.ppermute(block, axis, route)


def product(pattern, left_side, right_side):
    return jnp.einsum(pattern, left_side, right_side, preferred_element_type=jnp.float32)


def tile_place(position):
    tile_number = position // TILE
    return (tile_number // GW, tile_number % GW)


def window_mask(radius, query_time, query_col, query_row, key_time, key_col, key_row, key_valid):
    apart_time = jnp.abs(query_time[:, None] - key_time[None, :])
    apart_col = jnp.abs(query_col[:, None] - key_col[None, :])
    apart_row = jnp.abs(query_row[:, None] - key_row[None, :])
    inside = apart_time[None] <= radius[:, 0, None, None]
    inside = inside & (apart_row[None] <= radius[:, 1, None, None])
    inside = inside & (apart_col[None] <= radius[:, 2, None, None])
    return inside & key_valid[None, None, :]


def normalize(raw_rows, gain_full):
    as_float = raw_rows.astype(jnp.float32)
    inverse = lax.rsqrt(jnp.mean(as_float * as_float, axis=-1, keepdims=True) + EPSILON)
    return (as_float, inverse, (as_float * inverse * gain_full).astype(jnp.bfloat16))


def normalize_back(as_float, inverse, gain_full, d_normed):
    scaled = gain_full * d_normed
    inner = jnp.mean(scaled * as_float, axis=-1, keepdims=True)
    d_raw = inverse * scaled - as_float * (inverse * inverse * inverse) * inner
    return (d_raw.astype(jnp.bfloat16), jnp.sum(d_normed * as_float * inverse, axis=0))


def forward_group(query_part, key_part, value_part, allowed, scaling):
    scores = product("qhd,khd->hqk", query_part, key_part) * scaling
    scores = jnp.where(allowed, scores, NEG_FILL)
    row_max = jnp.max(scores, axis=2, keepdims=True)
    row_sum = jnp.sum(jnp.exp(scores - row_max), axis=2, keepdims=True)
    log_sum = row_max + jnp.log(row_sum)
    weights = jnp.exp(scores - log_sum)
    weights_low = weights.astype(jnp.bfloat16)
    mixed = product("hqk,khd->qhd", weights_low, value_part)
    return (weights, weights_low, mixed, log_sum[:, :, 0])


def score_grads(weights, output_part, value_part, delta, scaling):
    d_weights = product("qhd,khd->hqk", output_part, value_part)
    return (weights * (d_weights - delta[:, :, None]) * scaling).astype(jnp.bfloat16)


def attend_chunk(query_heads, output_heads, key_ext, value_ext, windows, masks, scaling, group_size):
    own_time, own_col, own_row, ext_time, ext_col, ext_row, ext_valid = masks
    heads = query_heads.shape[1]
    mixed_parts, dq_parts, dk_parts, dv_parts = ([], [], [], [])
    for first_head in range(0, heads, group_size):
        head_range = slice(first_head, first_head + group_size)
        allowed = window_mask(
            windows[head_range], own_time, own_col, own_row, ext_time, ext_col, ext_row, ext_valid
        )
        weights, weights_low, mixed, log_sum = forward_group(
            query_heads[:, head_range],
            key_ext[:, head_range],
            value_ext[:, head_range],
            allowed,
            scaling,
        )
        delta = jnp.sum(output_heads[:, head_range] * mixed, axis=2).T
        d_scores = score_grads(
            weights, output_heads[:, head_range], value_ext[:, head_range], delta, scaling
        )
        dq_parts.append(product("hqk,khd->qhd", d_scores, key_ext[:, head_range]))
        dk_parts.append(product("hqk,qhd->khd", d_scores, query_heads[:, head_range]))
        dv_parts.append(product("hqk,qhd->khd", weights_low, output_heads[:, head_range]))
        mixed_parts.append(mixed)
    rows = query_heads.shape[0]
    width = heads * HEAD
    return (
        jnp.concatenate(mixed_parts, axis=1).reshape(rows, width),
        jnp.concatenate(dq_parts, axis=1).reshape(rows, width),
        jnp.concatenate(dk_parts, axis=1).reshape(-1, width),
        jnp.concatenate(dv_parts, axis=1).reshape(-1, width),
    )


def shards(queries, key_vectors, value_vectors, windows, gain_query, gain_key, grad_output):
    tok_rows = queries.shape[1]
    width = HEADS * HEAD
    bounds = (0, 8, HEADS) if HEADS == 20 else (0, HEADS)
    chunks = len(bounds) - 1
    group_size = 4
    key_raw = key_vectors[0]
    value_local = value_vectors[0]
    extended = [
        padded(
            jnp.stack([key_raw[:, bounds[c] * HEAD : bounds[c + 1] * HEAD],
                       value_local[:, bounds[c] * HEAD : bounds[c + 1] * HEAD]]),
            (("sp", 1),),
            tok_rows,
        )
        for c in range(chunks)
    ]
    k_float = key_raw.astype(jnp.float32)
    k_inverse = lax.rsqrt(jnp.mean(k_float * k_float, axis=-1, keepdims=True) + EPSILON)
    gains = butterfly_gather(jnp.stack([gain_query, gain_key]), "fsdp")
    k_inverse, gains = lax.optimization_barrier((k_inverse, gains))
    inverse_ext = padded(k_inverse, (("sp", 0),), tok_rows)
    lo_inverse, hi_inverse = inverse_ext[:tok_rows], inverse_ext[2 * tok_rows :]
    gain_q_full, gain_k_full = gains[0], gains[1]
    my_index = lax.axis_index("sp")
    sp_count = lax.axis_size("sp")
    scaling = HEAD ** (-0.5)
    q_float, q_inverse, q_normed = normalize(queries[0], gain_q_full)
    k_normed = (k_float * k_inverse * gain_k_full).astype(jnp.bfloat16)
    output_local = grad_output[0]
    query_heads = q_normed.reshape(tok_rows, HEADS, HEAD)
    output_heads = output_local.reshape(tok_rows, HEADS, HEAD)
    own_pos = jnp.arange(tok_rows, dtype=jnp.int32)
    own_time, own_col = tile_place(own_pos)
    own_row = jnp.zeros((tok_rows,), jnp.int32) + my_index
    ext_pos = jnp.arange(3 * tok_rows, dtype=jnp.int32)
    ext_time, ext_col = tile_place(ext_pos % tok_rows)
    ext_row = my_index - 1 + ext_pos // tok_rows
    ext_valid = (ext_row >= 0) & (ext_row < sp_count)
    masks = (own_time, own_col, own_row, ext_time, ext_col, ext_row, ext_valid)
    middle = slice(tok_rows, 2 * tok_rows)
    results, received, near_dg = [], [], []
    for c in range(chunks):
        if c > 0:
            extended[c], held = lax.optimization_barrier((extended[c], sent))
        cols = slice(bounds[c] * HEAD, bounds[c + 1] * HEAD)
        heads = slice(bounds[c], bounds[c + 1])
        chunk_heads = bounds[c + 1] - bounds[c]
        lo_float = extended[c][0, :tok_rows].astype(jnp.float32)
        hi_float = extended[c][0, 2 * tok_rows :].astype(jnp.float32)
        gain_c = gain_k_full[cols]
        key_ext = jnp.concatenate([
            (lo_float * lo_inverse * gain_c).astype(jnp.bfloat16),
            k_normed[:, cols],
            (hi_float * hi_inverse * gain_c).astype(jnp.bfloat16),
        ]).reshape(3 * tok_rows, chunk_heads, HEAD)
        value_ext = extended[c][1].reshape(3 * tok_rows, chunk_heads, HEAD)
        mixed_c, dq_c, dk_c, dv_c = attend_chunk(
            query_heads[:, heads], output_heads[:, heads], key_ext, value_ext,
            windows[heads], masks, scaling, group_size,
        )
        lower_send = jnp.stack([dk_c[:tok_rows], dv_c[:tok_rows]]).astype(jnp.bfloat16)
        upper_send = jnp.stack([dk_c[2 * tok_rows :], dv_c[2 * tok_rows :]]).astype(jnp.bfloat16)
        received.append((passed_along(lower_send, "sp", -1), passed_along(upper_send, "sp", 1)))
        sent = (lower_send, upper_send)
        results.append((mixed_c, dq_c, dk_c[middle], dv_c[middle]))
        near_dg.append(
            jnp.sum(lower_send[0].astype(jnp.float32) * lo_float * lo_inverse, axis=0)
            + jnp.sum(upper_send[0].astype(jnp.float32) * hi_float * hi_inverse, axis=0)
        )
    mixed_all = jnp.concatenate([r[0] for r in results], axis=1)
    dq_normed = jnp.concatenate([r[1] for r in results], axis=1)
    dk_own = jnp.concatenate([r[2] for r in results], axis=1)
    dv_own = jnp.concatenate([r[3] for r in results], axis=1)
    dq_out, dg_query = normalize_back(q_float, q_inverse, gain_q_full, dq_normed)
    dg_key = jnp.sum(dk_own * k_float * k_inverse, axis=0) + jnp.concatenate(near_dg)
    all_tokens = tok_rows * sp_count * lax.axis_size("clip") * lax.axis_size("fsdp")
    factor = all_tokens ** (-0.5)
    sizes = {axis: lax.axis_size(axis) for axis in ("fsdp", "clip", "sp")}
    partial_sums = jnp.stack([dg_query, dg_key])
    if all(count & (count - 1) == 0 for count in sizes.values()):
        steps = bits_of([("clip", sizes["clip"])]) + [("sp", 1)] * (sizes["sp"] > 1)
        steps += bits_of([("fsdp", sizes["fsdp"])])
        steps += [("sp", bit) for _, bit in bits_of([("sp", sizes["sp"])]) if bit > 1]
        totals = butterfly_sum(partial_sums, steps[:-1])
        received, totals = lax.optimization_barrier((received, totals))
        totals = butterfly_sum(totals, steps[-1:])
    else:
        totals = lax.psum(partial_sums, ("fsdp", "clip", "sp"))
        received, totals = lax.optimization_barrier((received, totals))
    lower = jnp.concatenate([r[0] for r in received], axis=2).astype(jnp.float32)
    upper = jnp.concatenate([r[1] for r in received], axis=2).astype(jnp.float32)
    dk_normed = dk_own + lower[0] + upper[0]
    dv_total = dv_own + lower[1] + upper[1]
    dk_out, _ = normalize_back(k_float, k_inverse, gain_k_full, dk_normed)
    share = gain_query.shape[0]
    totals = lax.dynamic_slice_in_dim(totals, lax.axis_index("fsdp") * share, share, axis=1)
    return (
        mixed_all.astype(jnp.bfloat16)[None],
        dq_out[None],
        dk_out[None],
        dv_total.astype(jnp.bfloat16)[None],
        totals[0] * factor,
        totals[1] * factor,
    )


def solution(mesh):
    return jax.shard_map(
        shards,
        mesh=mesh,
        in_specs=(
            P(("clip", "fsdp"), "sp", None),
            P(("clip", "fsdp"), "sp", None),
            P(("clip", "fsdp"), "sp", None),
            P(),
            P("fsdp"),
            P("fsdp"),
            P(("clip", "fsdp"), "sp", None),
        ),
        out_specs=(
            P(("clip", "fsdp"), "sp", None),
            P(("clip", "fsdp"), "sp", None),
            P(("clip", "fsdp"), "sp", None),
            P(("clip", "fsdp"), "sp", None),
            P("fsdp"),
            P("fsdp"),
        ),
        check_vma=False,
    )
```
